32 devices in a mesh: wl: 2 (over y), row: 16 (over z, x, core).
Axes of the slice: x: 2, y: 2, z: 4, core: 2. Of those that a mesh axis runs over, the one named last changes fastest.
Arguments:
- scenes: float32 [2, 4096, 4096], P(None, 'row'), may hold values from -6 to 6
- optics: bfloat16 [4, 2, 4096, 4096], P('wl', None, 'row'), may hold values from -4 to 4
- weights: float32 [4, 2], replicated, may hold values from 0.1 to 2
Outputs:
- blurred: float32 [2, 4096, 4096], P(None, 'row', 'wl')
The draws below stay inside these ranges and needn't reach their ends.
All inputs are finite; a program needn't handle non-finite values.
Results may differ from the reference program's by a relative error of at most 0.0003.
Values may be sent and summed in bfloat16 or wider, within the bound.
No kernel may reach another device: no remote copies, remote signals or barrier semaphores. Data moves between devices by JAX's collectives and lax.ppermute only.
A program may use at most 128 MiB of HBM per device.

```python
import math
import jax
import jax.numpy as jnp
from jax import lax

N = 4096
WAVES = 4


def block_levels(rng, shape, pieces, smallest, high):
    gain, own = 1.0, jax.random.fold_in(rng, 6)
    for axis_at, blocks in pieces:
        steps = jnp.exp(jax.random.uniform(jax.random.fold_in(own, axis_at), (blocks,), jnp.float32, smallest / len(pieces), high / len(pieces)))
        gain = gain * jnp.repeat(steps, shape[axis_at] // blocks).reshape([-1 if axis == axis_at else 1 for axis in range(len(shape))])
    return gain


def bell_draw(rng, extent, spread, bound, pieces=(), kind=jnp.bfloat16):
    result = jax.random.normal(rng, extent, jnp.float32) * spread
    if len(pieces) > 0:
        result = block_levels(rng, extent, pieces, -0.22, 0.18) * result
    return jnp.clip(result, min=-bound, max=bound).astype(kind)


def setup_inputs(seed: int = 0) -> dict:
    seeds = jax.random.split(jax.random.key(seed), 4)
    return {
        "scenes": bell_draw(seeds[0], (2, N, N), 1.0, 6.0, ((1, 16),), jnp.float32),
        "optics": bell_draw(seeds[1], (WAVES, 2, N, N), 0.7, 4.0, ((0, 2), (2, 16))),
        "weights": jnp.clip(jnp.exp(jax.random.uniform(seeds[2], (WAVES, 2), jnp.float32, math.log(0.1), math.log(2.0))), 0.1, 2.0),
    }


def reference(scenes, optics, weights):
    field = lax.complex(scenes[0], scenes[1])
    spectrum = jnp.fft.fft2(field)
    mirrored = jnp.conj(jnp.roll(jnp.flip(spectrum, (0, 1)), 1, (0, 1)))
    even_part = (spectrum + mirrored) * 0.5
    odd_part = (spectrum - mirrored) * 0.5
    combined = jnp.zeros_like(spectrum)
    for colour in range(WAVES):
        response = lax.complex(optics[colour, 0].astype(jnp.float32), optics[colour, 1].astype(jnp.float32))
        combined = combined + response * (weights[colour, 0] * even_part + weights[colour, 1] * odd_part)
    result_image = jnp.fft.ifft2(combined)
    return jnp.stack([jnp.real(result_image), jnp.imag(result_image)])
```

```python
import math

import jax
import jax.numpy as jnp
from jax import lax
from jax.sharding import PartitionSpec as P

PRECISE = lax.Precision.HIGHEST


def phase_table(height, across, modulus, orient):
    left_ids = lax.broadcasted_iota(jnp.int32, (height, across), 0)
    right_ids = lax.broadcasted_iota(jnp.int32, (height, across), 1)
    turns = (left_ids * right_ids % modulus).astype(jnp.float32)
    angles = turns * (orient * 2.0 * math.pi / modulus)
    return (jnp.cos(angles), jnp.sin(angles))


def block_table(cos_part, sin_part):
    upper = jnp.stack([cos_part, -sin_part])
    lower = jnp.stack([sin_part, cos_part])
    return jnp.stack([upper, lower])


def transform_last(stacked, orient):
    rows_here = stacked.shape[1]
    length = stacked.shape[2]
    narrow = 32
    across = length // narrow
    small_cos, small_sin = phase_table(narrow, narrow, narrow, orient)
    twist_cos, twist_sin = phase_table(narrow, across, length, orient)
    large_cos, large_sin = phase_table(across, across, across, orient)
    small_block = jnp.transpose(block_table(small_cos, small_sin), (0, 2, 1, 3))
    large_block = jnp.transpose(block_table(large_cos, large_sin), (1, 2, 0, 3))
    grid = stacked.reshape((2, rows_here, narrow, across))
    first = jnp.einsum("cadb,drbn->cran", small_block, grid, precision=PRECISE)
    turned_real = first[0] * twist_cos - first[1] * twist_sin
    turned_imag = first[0] * twist_sin + first[1] * twist_cos
    turned = jnp.stack([turned_real, turned_imag])
    second = jnp.einsum("dran,dnck->crak", turned, large_block, precision=PRECISE)
    return jnp.swapaxes(second, -1, -2).reshape((2, rows_here, length))


def flip_freq(values_in):
    return jnp.roll(jnp.flip(values_in, -1), 1, -1)


def to_pairs(values_in, group_count):
    length = values_in.shape[-1]
    midpoint = length // 2
    pair_span = midpoint // group_count
    leading = values_in.shape[:-1]
    lower_part = values_in[..., :midpoint].reshape(leading + (group_count, pair_span))
    mirror_part = flip_freq(values_in[..., midpoint:]).reshape(leading + (group_count, pair_span))
    return jnp.stack([lower_part, mirror_part], -2).reshape(leading + (length,))


def from_pairs(values_in, group_count):
    length = values_in.shape[-1]
    midpoint = length // 2
    pair_span = midpoint // group_count
    leading = values_in.shape[:-1]
    grouped = values_in.reshape(leading + (group_count, 2, pair_span))
    lower_part = grouped[..., 0, :].reshape(leading + (midpoint,))
    mirror_part = grouped[..., 1, :].reshape(leading + (midpoint,))
    upper_part = jnp.flip(jnp.roll(mirror_part, -1, -1), -1)
    return jnp.concatenate([lower_part, upper_part], -1)


def untangle_combine(spec_real, spec_imag, optic_pairs, weight_rows, first_group, pair_span):
    slot_ids = lax.broadcasted_iota(jnp.int32, (2 * pair_span, 1), 0)
    itself = jnp.logical_and(first_group, slot_ids % pair_span == 0)
    swapped_real = jnp.concatenate([spec_real[pair_span:], spec_real[:pair_span]], 0)
    swapped_imag = jnp.concatenate([spec_imag[pair_span:], spec_imag[:pair_span]], 0)
    partner_real = jnp.where(itself, spec_real, swapped_real)
    partner_imag = jnp.where(itself, spec_imag, swapped_imag)
    mirror_real = flip_freq(partner_real)
    mirror_imag = -flip_freq(partner_imag)
    even_real = 0.5 * (spec_real + mirror_real)
    even_imag = 0.5 * (spec_imag + mirror_imag)
    odd_real = 0.5 * (spec_real - mirror_real)
    odd_imag = 0.5 * (spec_imag - mirror_imag)
    combined_real = jnp.zeros_like(spec_real)
    combined_imag = jnp.zeros_like(spec_imag)
    for colour in range(optic_pairs.shape[0]):
        mixed_real = weight_rows[colour, 0] * even_real + weight_rows[colour, 1] * odd_real
        mixed_imag = weight_rows[colour, 0] * even_imag + weight_rows[colour, 1] * odd_imag
        resp_real = optic_pairs[colour, 0].astype(jnp.float32)
        resp_imag = optic_pairs[colour, 1].astype(jnp.float32)
        combined_real = combined_real + resp_real * mixed_real - resp_imag * mixed_imag
        combined_imag = combined_imag + resp_real * mixed_imag + resp_imag * mixed_real
    return (combined_real, combined_imag)


def local(scenes, optics, weights):
    row_count = lax.axis_size("row")
    length = scenes.shape[2]
    midpoint = length // 2
    pair_span = midpoint // row_count
    norm_factor = 1.0 / (float(length) * float(length))
    wl_index = lax.axis_index("wl")
    local_waves = optics.shape[0]
    weight_rows = lax.dynamic_slice_in_dim(weights, wl_index * local_waves, local_waves, 0)
    first_row = lax.axis_index("row") == 0
    cols = transform_last(scenes, -1.0)
    paired = to_pairs(cols, row_count)
    columns_moved = jnp.swapaxes(
        lax.all_to_all(paired, "row", split_axis=2, concat_axis=1, tiled=True), 1, 2
    )
    spec = transform_last(columns_moved, -1.0)
    optic_pairs = lax.all_to_all(
        to_pairs(optics, row_count), "row", split_axis=3, concat_axis=2, tiled=True
    )
    optic_pairs = jnp.swapaxes(optic_pairs, 2, 3)
    combined_real, combined_imag = untangle_combine(
        spec[0], spec[1], optic_pairs, weight_rows, first_row, pair_span
    )
    back = transform_last(jnp.stack([combined_real, combined_imag]), 1.0)
    returned = lax.all_to_all(back, "row", split_axis=2, concat_axis=1, tiled=True)
    returned = from_pairs(jnp.swapaxes(returned, 1, 2), row_count)
    result_image = transform_last(returned, 1.0) * norm_factor
    return lax.psum_scatter(result_image, "wl", scatter_dimension=2, tiled=True)


def solution(mesh):
    in_specs = (P(None, "row", None), P("wl", None, "row", None), P())
    out_specs = P(None, "row", "wl")
    return jax.shard_map(local, mesh=mesh, in_specs=in_specs, out_specs=out_specs, check_vma=False)
```

```python
import math

import jax
import jax.numpy as jnp
from jax import lax
from jax.sharding import PartitionSpec as P

PRECISE = lax.Precision.HIGHEST
NARROW = 32


def phase(left_ids, right_ids, modulus, orient):
    turns = (left_ids * right_ids % modulus).astype(jnp.float32)
    angles = turns * (orient * 2.0 * math.pi / modulus)
    return (jnp.cos(angles), jnp.sin(angles))


def ids(count):
    return jnp.arange(count, dtype=jnp.int32)


def cblock(cos_part, sin_part):
    return jnp.stack([jnp.stack([cos_part, -sin_part]), jnp.stack([sin_part, cos_part])])


def small_tables(out_count, in_count, modulus, orients):
    tables = []
    for orient in orients:
        cos_part, sin_part = phase(ids(out_count)[:, None], ids(in_count)[None, :], modulus, orient)
        tables.append(cblock(cos_part, sin_part))
    return jnp.stack(tables)


def twist(values, axis_e, cos_part, sin_part):
    real = jnp.take(values, 0, axis=axis_e)
    imag = jnp.take(values, 1, axis=axis_e)
    return jnp.stack([real * cos_part - imag * sin_part, real * sin_part + imag * cos_part], axis_e)


def canon_to_groups(canon, group_count):
    mcount, span_c = canon.shape[0], canon.shape[-1] // 2
    mid = canon.shape[1:-1]
    if group_count == mcount:
        return canon
    span = mcount * span_c // group_count
    flat = jnp.moveaxis(canon.reshape((mcount,) + mid + (2, span_c)), 0, -2)
    flat = flat.reshape(mid + (2, group_count, span))
    return jnp.moveaxis(flat, -2, 0).reshape((group_count,) + mid + (2 * span,))


def groups_to_canon(grouped, mcount, axis_g):
    group_count = grouped.shape[axis_g]
    if group_count == mcount:
        return grouped
    moved = jnp.moveaxis(grouped, axis_g, 0)
    mid = moved.shape[1:-1]
    span = moved.shape[-1] // 2
    span_c = group_count * span // mcount
    flat = jnp.moveaxis(moved.reshape((group_count,) + mid + (2, span)), 0, -2)
    flat = flat.reshape(mid + (2, mcount, span_c))
    canon = jnp.moveaxis(flat, -2, 0).reshape((mcount,) + mid + (2 * span_c,))
    return jnp.moveaxis(canon, 0, axis_g)


def forward_rows(scenes):
    rows_here, length = scenes.shape[1], scenes.shape[2]
    across = length // NARROW
    half_k = across // 2
    grid = scenes.reshape((2, rows_here, NARROW, across))
    first_tab = jnp.transpose(small_tables(NARROW, NARROW, NARROW, (-1.0, 1.0)), (0, 3, 1, 2, 4))
    first = jnp.einsum("oaedb,drbn->oaern", first_tab, grid, precision=PRECISE)
    tw_cos, tw_sin = [], []
    for orient in (-1.0, 1.0):
        cos_part, sin_part = phase(ids(NARROW)[:, None], ids(across)[None, :], length, orient)
        tw_cos.append(cos_part)
        tw_sin.append(sin_part)
    tw_cos = jnp.stack(tw_cos)[:, :, None, :]
    tw_sin = jnp.stack(tw_sin)[:, :, None, :]
    turned = twist(first, 2, tw_cos, tw_sin)
    second_tab = jnp.transpose(small_tables(half_k, across, across, (-1.0, 1.0)), (0, 2, 4, 1, 3))
    second = jnp.einsum("oaern,oenfk->oarfk", turned, second_tab, precision=PRECISE)
    signs = 1.0 - 2.0 * (ids(across) % 2).astype(jnp.float32)
    nyquist = jnp.einsum("ern,n->er", first[0, 0], signs, precision=PRECISE)
    per_block = across // NARROW
    mcount = half_k // per_block
    blocks = second.reshape((2, NARROW, rows_here, 2, mcount, per_block))
    canon = jnp.transpose(blocks, (4, 3, 2, 0, 5, 1)).reshape((mcount, 2, rows_here, 2 * across))
    canon = canon.at[0, :, :, across].set(nyquist)
    return canon


def forward_cols(columns):
    length, width = columns.shape[1], columns.shape[2]
    across = length // NARROW
    grid = columns.reshape((2, NARROW, across, width))
    first_tab = jnp.transpose(small_tables(NARROW, NARROW, NARROW, (-1.0, 1.0)), (0, 3, 1, 2, 4))
    first = jnp.einsum("oafeb,ebnj->oafnj", first_tab, grid, precision=PRECISE)
    tw_cos, tw_sin = [], []
    for orient in (-1.0, 1.0):
        cos_part, sin_part = phase(ids(NARROW)[:, None], ids(across)[None, :], length, orient)
        tw_cos.append(cos_part)
        tw_sin.append(sin_part)
    tw_cos = jnp.stack(tw_cos)[:, :, :, None]
    tw_sin = jnp.stack(tw_sin)[:, :, :, None]
    turned = twist(first, 2, tw_cos, tw_sin)
    second_tab = small_tables(across, across, across, (-1.0, 1.0))
    second = jnp.einsum("ofekn,oaenj->ofkaj", second_tab, turned, precision=PRECISE)
    return second.reshape((2, 2, length, width))


def inverse_cols(combined):
    length, width = combined.shape[1], combined.shape[2]
    across = length // NARROW
    grid = combined.reshape((2, NARROW, across, width))
    first_tab = jnp.transpose(small_tables(NARROW, NARROW, NARROW, (1.0,))[0], (2, 0, 1, 3))
    first = jnp.einsum("afeb,ebnj->afnj", first_tab, grid, precision=PRECISE)
    cos_part, sin_part = phase(ids(NARROW)[:, None], ids(across)[None, :], length, 1.0)
    turned = twist(first, 1, cos_part[:, :, None], sin_part[:, :, None])
    second_tab = jnp.transpose(small_tables(across, across, across, (1.0,))[0], (0, 2, 1, 3))
    second = jnp.einsum("fken,aenj->fkaj", second_tab, turned, precision=PRECISE)
    return second.reshape((2, length, width))


def inverse_rows(canon, length, scale):
    mcount, rows_here, width = canon.shape[1], canon.shape[2], canon.shape[3]
    across = width // 2
    first_tab = jnp.transpose(small_tables(NARROW, mcount, NARROW, (1.0, -1.0)), (0, 3, 1, 2, 4))
    first = jnp.einsum("oafem,emRj->oafRj", first_tab, canon, precision=PRECISE)
    lower = first[0, :, :, :, :across]
    upper = first[1, :, :, :, across:]
    flip_gain = -2.0 * (ids(NARROW) % 2).astype(jnp.float32)
    fix = flip_gain[:, None, None] * canon[:, 0, :, across][None]
    lane0 = (ids(across) == 0)[None, None, None, :]
    upper = jnp.where(lane0, upper + fix[..., None], upper)
    cos_up, sin_up = phase(ids(NARROW)[:, None], ids(across)[None, :], length, 1.0)
    cos_dn, sin_dn = phase(ids(NARROW)[:, None], ids(across)[None, :], length, -1.0)
    lower = twist(lower, 1, cos_up[:, None, :], sin_up[:, None, :])
    upper = twist(upper, 1, cos_dn[:, None, :], sin_dn[:, None, :])
    tabs = small_tables(across, across, across, (1.0, -1.0)) * scale
    tabs = jnp.transpose(tabs, (0, 2, 4, 1, 3))
    out = jnp.einsum("aeRu,eufk->aRfk", lower, tabs[0], precision=PRECISE)
    out = out + jnp.einsum("aeRu,eufk->aRfk", upper, tabs[1], precision=PRECISE)
    return jnp.transpose(out, (2, 1, 3, 0)).reshape((2, rows_here, length))


def pair_optics(optics):
    length = optics.shape[-1]
    across = length // NARROW
    half = length // 2
    mcount = half // across
    block = [lax.slice_in_dim(optics, across * i, across * (i + 1), axis=3) for i in range(NARROW)]
    windows = []
    for m in range(mcount):
        second = block[(half // across) if m == 0 else (NARROW - m)]
        windows.append(jnp.concatenate([block[NARROW - 1 - m], second], -1))
    windows = jnp.stack(windows)
    src = ids(2 * across)[:, None]
    dst = ids(across)[None, :]
    picker = jnp.logical_or(
        jnp.logical_and(src == across - dst, dst > 0), jnp.logical_and(src == across, dst == 0)
    ).astype(optics.dtype)
    mirrored = jnp.einsum("mwcpv,vu->mwcpu", windows, picker, preferred_element_type=jnp.float32)
    lower = jnp.stack(block[:mcount])
    return jnp.concatenate([lower, mirrored.astype(optics.dtype)], -1)


def local(scenes, optics, weights):
    row_count = lax.axis_size("row")
    length = scenes.shape[2]
    across = length // NARROW
    norm_factor = 1.0 / (float(length) * float(length))
    wl_index = lax.axis_index("wl")
    local_waves = optics.shape[0]
    weight_rows = lax.dynamic_slice_in_dim(weights, wl_index * local_waves, local_waves, 0)
    first_row = lax.axis_index("row") == 0

    canon = forward_rows(scenes)
    mcount = canon.shape[0]
    sent = canon_to_groups(canon, row_count)
    got = lax.all_to_all(sent, "row", split_axis=0, concat_axis=2, tiled=True)[0]
    spec = forward_cols(got)

    optic_canon = pair_optics(optics)
    optic_sent = canon_to_groups(optic_canon, row_count)
    optic_got = lax.all_to_all(optic_sent, "row", split_axis=0, concat_axis=3, tiled=True)[0]

    width = spec.shape[-1]
    span = width // 2
    lane_ids = ids(width)
    itself = jnp.logical_and(first_row, lane_ids % span == 0)
    direct = spec[0]
    flipped = spec[1]
    swapped = jnp.concatenate([flipped[..., span:], flipped[..., :span]], -1)
    partner = jnp.where(itself, flipped, swapped)
    mirror_real = partner[0]
    mirror_imag = -partner[1]
    even_real = 0.5 * (direct[0] + mirror_real)
    even_imag = 0.5 * (direct[1] + mirror_imag)
    odd_real = 0.5 * (direct[0] - mirror_real)
    odd_imag = 0.5 * (direct[1] - mirror_imag)
    combined_real = jnp.zeros_like(even_real)
    combined_imag = jnp.zeros_like(even_imag)
    for colour in range(local_waves):
        mixed_real = weight_rows[colour, 0] * even_real + weight_rows[colour, 1] * odd_real
        mixed_imag = weight_rows[colour, 0] * even_imag + weight_rows[colour, 1] * odd_imag
        resp_real = optic_got[colour, 0].astype(jnp.float32)
        resp_imag = optic_got[colour, 1].astype(jnp.float32)
        combined_real = combined_real + resp_real * mixed_real - resp_imag * mixed_imag
        combined_imag = combined_imag + resp_real * mixed_imag + resp_imag * mixed_real

    back = inverse_cols(jnp.stack([combined_real, combined_imag]))
    rows_here = length // row_count
    back = back.reshape((2, row_count, rows_here, width))
    returned = lax.all_to_all(back, "row", split_axis=1, concat_axis=1, tiled=True)
    returned = groups_to_canon(returned, mcount, 1)
    result_image = inverse_rows(returned, length, norm_factor)
    return lax.psum_scatter(result_image, "wl", scatter_dimension=2, tiled=True)


def solution(mesh):
    in_specs = (P(None, "row", None), P("wl", None, "row", None), P())
    out_specs = P(None, "row", "wl")
    return jax.shard_map(local, mesh=mesh, in_specs=in_specs, out_specs=out_specs, check_vma=False)
```

```python
import math

import jax
import jax.numpy as jnp
from jax import lax
from jax.sharding import PartitionSpec as P

PRECISE = lax.Precision.HIGHEST
NARROW = 32


def phase(left_ids, right_ids, modulus, orient):
    turns = (left_ids * right_ids % modulus).astype(jnp.float32)
    angles = turns * (orient * 2.0 * math.pi / modulus)
    return (jnp.cos(angles), jnp.sin(angles))


def ids(count):
    return jnp.arange(count, dtype=jnp.int32)


def cblock(cos_part, sin_part):
    return jnp.stack([jnp.stack([cos_part, -sin_part]), jnp.stack([sin_part, cos_part])])


def small_tables(out_count, in_count, modulus, orients):
    tables = []
    for orient in orients:
        cos_part, sin_part = phase(ids(out_count)[:, None], ids(in_count)[None, :], modulus, orient)
        tables.append(cblock(cos_part, sin_part))
    return jnp.stack(tables)


def twist(values, axis_e, cos_part, sin_part):
    real = jnp.take(values, 0, axis=axis_e)
    imag = jnp.take(values, 1, axis=axis_e)
    return jnp.stack([real * cos_part - imag * sin_part, real * sin_part + imag * cos_part], axis_e)


def canon_to_groups(canon, group_count):
    mcount, span_c = canon.shape[0], canon.shape[-1] // 2
    mid = canon.shape[1:-1]
    if group_count == mcount:
        return canon
    span = mcount * span_c // group_count
    flat = jnp.moveaxis(canon.reshape((mcount,) + mid + (2, span_c)), 0, -2)
    flat = flat.reshape(mid + (2, group_count, span))
    return jnp.moveaxis(flat, -2, 0).reshape((group_count,) + mid + (2 * span,))


def groups_to_canon(grouped, mcount, axis_g):
    group_count = grouped.shape[axis_g]
    if group_count == mcount:
        return grouped
    moved = jnp.moveaxis(grouped, axis_g, 0)
    mid = moved.shape[1:-1]
    span = moved.shape[-1] // 2
    span_c = group_count * span // mcount
    flat = jnp.moveaxis(moved.reshape((group_count,) + mid + (2, span)), 0, -2)
    flat = flat.reshape(mid + (2, mcount, span_c))
    canon = jnp.moveaxis(flat, -2, 0).reshape((mcount,) + mid + (2 * span_c,))
    return jnp.moveaxis(canon, 0, axis_g)


def forward_rows(scenes):
    rows_here, length = scenes.shape[1], scenes.shape[2]
    across = length // NARROW
    half_k = across // 2
    grid = scenes.reshape((2, rows_here, NARROW, across))
    first_tab = jnp.transpose(small_tables(NARROW, NARROW, NARROW, (-1.0, 1.0)), (0, 3, 1, 2, 4))
    first = jnp.einsum("oaedb,drbn->oaern", first_tab, grid, precision=PRECISE)
    tw_cos, tw_sin = [], []
    for orient in (-1.0, 1.0):
        cos_part, sin_part = phase(ids(NARROW)[:, None], ids(across)[None, :], length, orient)
        tw_cos.append(cos_part)
        tw_sin.append(sin_part)
    tw_cos = jnp.stack(tw_cos)[:, :, None, :]
    tw_sin = jnp.stack(tw_sin)[:, :, None, :]
    turned = twist(first, 2, tw_cos, tw_sin)
    second_tab = jnp.transpose(small_tables(half_k, across, across, (-1.0, 1.0)), (0, 2, 4, 1, 3))
    second = jnp.einsum("oaern,oenfk->oarfk", turned, second_tab, precision=PRECISE)
    signs = 1.0 - 2.0 * (ids(across) % 2).astype(jnp.float32)
    nyquist = jnp.einsum("ern,n->er", first[0, 0], signs, precision=PRECISE)
    per_block = across // NARROW
    mcount = half_k // per_block
    blocks = second.reshape((2, NARROW, rows_here, 2, mcount, per_block))
    canon = jnp.transpose(blocks, (4, 3, 2, 0, 5, 1)).reshape((mcount, 2, rows_here, 2 * across))
    canon = canon.at[0, :, :, across].set(nyquist)
    return canon


def forward_cols(columns):
    length, width = columns.shape[1], columns.shape[2]
    across = length // NARROW
    grid = columns.reshape((2, NARROW, across, width))
    first_tab = jnp.transpose(small_tables(NARROW, NARROW, NARROW, (-1.0, 1.0)), (0, 3, 1, 2, 4))
    first = jnp.einsum("oafeb,ebnj->oafnj", first_tab, grid, precision=PRECISE)
    tw_cos, tw_sin = [], []
    for orient in (-1.0, 1.0):
        cos_part, sin_part = phase(ids(NARROW)[:, None], ids(across)[None, :], length, orient)
        tw_cos.append(cos_part)
        tw_sin.append(sin_part)
    tw_cos = jnp.stack(tw_cos)[:, :, :, None]
    tw_sin = jnp.stack(tw_sin)[:, :, :, None]
    turned = twist(first, 2, tw_cos, tw_sin)
    second_tab = small_tables(across, across, across, (-1.0, 1.0))
    second = jnp.einsum("ofekn,oaenj->ofkaj", second_tab, turned, precision=PRECISE)
    return second.reshape((2, 2, length, width))


def inverse_cols(combined):
    length, width = combined.shape[1], combined.shape[2]
    across = length // NARROW
    grid = combined.reshape((2, NARROW, across, width))
    first_tab = jnp.transpose(small_tables(NARROW, NARROW, NARROW, (1.0,))[0], (2, 0, 1, 3))
    first = jnp.einsum("afeb,ebnj->afnj", first_tab, grid, precision=PRECISE)
    cos_part, sin_part = phase(ids(NARROW)[:, None], ids(across)[None, :], length, 1.0)
    turned = twist(first, 1, cos_part[:, :, None], sin_part[:, :, None])
    second_tab = jnp.transpose(small_tables(across, across, across, (1.0,))[0], (0, 2, 1, 3))
    second = jnp.einsum("fken,aenj->fkaj", second_tab, turned, precision=PRECISE)
    return second.reshape((2, length, width))


def inverse_rows(canon, length, scale):
    mcount, rows_here, width = canon.shape[1], canon.shape[2], canon.shape[3]
    across = width // 2
    first_tab = jnp.transpose(small_tables(NARROW, mcount, NARROW, (1.0, -1.0)), (0, 3, 1, 2, 4))
    first = jnp.einsum("oafem,emRj->oafRj", first_tab, canon, precision=PRECISE)
    lower = first[0, :, :, :, :across]
    upper = first[1, :, :, :, across:]
    flip_gain = -2.0 * (ids(NARROW) % 2).astype(jnp.float32)
    fix = flip_gain[:, None, None] * canon[:, 0, :, across][None]
    lane0 = (ids(across) == 0)[None, None, None, :]
    upper = jnp.where(lane0, upper + fix[..., None], upper)
    cos_up, sin_up = phase(ids(NARROW)[:, None], ids(across)[None, :], length, 1.0)
    cos_dn, sin_dn = phase(ids(NARROW)[:, None], ids(across)[None, :], length, -1.0)
    lower = twist(lower, 1, cos_up[:, None, :], sin_up[:, None, :])
    upper = twist(upper, 1, cos_dn[:, None, :], sin_dn[:, None, :])
    tabs = small_tables(across, across, across, (1.0, -1.0)) * scale
    tabs = jnp.transpose(tabs, (0, 2, 4, 1, 3))
    out = jnp.einsum("aeRu,eufk->aRfk", lower, tabs[0], precision=PRECISE)
    out = out + jnp.einsum("aeRu,eufk->aRfk", upper, tabs[1], precision=PRECISE)
    return jnp.transpose(out, (2, 1, 3, 0)).reshape((2, rows_here, length))


def pair_optics(optics):
    length = optics.shape[-1]
    across = length // NARROW
    half = length // 2
    mcount = half // across
    block = [lax.slice_in_dim(optics, across * i, across * (i + 1), axis=3) for i in range(NARROW)]
    windows = []
    for m in range(mcount):
        second = block[(half // across) if m == 0 else (NARROW - m)]
        windows.append(jnp.concatenate([block[NARROW - 1 - m], second], -1))
    windows = jnp.stack(windows)
    src = ids(2 * across)[:, None]
    dst = ids(across)[None, :]
    picker = jnp.logical_or(
        jnp.logical_and(src == across - dst, dst > 0), jnp.logical_and(src == across, dst == 0)
    ).astype(optics.dtype)
    mirrored = jnp.einsum("mwcpv,vu->mwcpu", windows, picker, preferred_element_type=jnp.float32)
    lower = jnp.stack(block[:mcount])
    return jnp.concatenate([lower, mirrored.astype(optics.dtype)], -1)


def local(scenes, optics, weights):
    row_count = lax.axis_size("row")
    length = scenes.shape[2]
    across = length // NARROW
    norm_factor = 1.0 / (float(length) * float(length))
    wl_index = lax.axis_index("wl")
    local_waves = optics.shape[0]
    weight_rows = lax.dynamic_slice_in_dim(weights, wl_index * local_waves, local_waves, 0)
    first_row = lax.axis_index("row") == 0

    optic_canon = pair_optics(optics)
    optic_sent = canon_to_groups(optic_canon, row_count)
    optic_got = lax.all_to_all(optic_sent, "row", split_axis=0, concat_axis=3, tiled=True)[0]

    canon = forward_rows(scenes)
    mcount = canon.shape[0]
    sent = canon_to_groups(canon, row_count)
    optic_got, sent = lax.optimization_barrier((optic_got, sent))
    got = lax.all_to_all(sent, "row", split_axis=0, concat_axis=2, tiled=True)[0]
    spec = forward_cols(got)

    width = spec.shape[-1]
    span = width // 2
    lane_ids = ids(width)
    itself = jnp.logical_and(first_row, lane_ids % span == 0)
    direct = spec[0]
    flipped = spec[1]
    swapped = jnp.concatenate([flipped[..., span:], flipped[..., :span]], -1)
    partner = jnp.where(itself, flipped, swapped)
    mirror_real = partner[0]
    mirror_imag = -partner[1]
    even_real = 0.5 * (direct[0] + mirror_real)
    even_imag = 0.5 * (direct[1] + mirror_imag)
    odd_real = 0.5 * (direct[0] - mirror_real)
    odd_imag = 0.5 * (direct[1] - mirror_imag)
    combined_real = jnp.zeros_like(even_real)
    combined_imag = jnp.zeros_like(even_imag)
    for colour in range(local_waves):
        mixed_real = weight_rows[colour, 0] * even_real + weight_rows[colour, 1] * odd_real
        mixed_imag = weight_rows[colour, 0] * even_imag + weight_rows[colour, 1] * odd_imag
        resp_real = optic_got[colour, 0].astype(jnp.float32)
        resp_imag = optic_got[colour, 1].astype(jnp.float32)
        combined_real = combined_real + resp_real * mixed_real - resp_imag * mixed_imag
        combined_imag = combined_imag + resp_real * mixed_imag + resp_imag * mixed_real

    back = inverse_cols(jnp.stack([combined_real, combined_imag]))
    rows_here = length // row_count
    back = back.reshape((2, row_count, rows_here, width))
    returned = lax.all_to_all(back, "row", split_axis=1, concat_axis=1, tiled=True)
    returned = groups_to_canon(returned, mcount, 1)
    result_image = inverse_rows(returned, length, norm_factor)
    wl_count = lax.axis_size("wl")
    if wl_count != 2:
        return lax.psum_scatter(result_image, "wl", scatter_dimension=2, tiled=True)
    half = length // 2
    kept = lax.dynamic_slice_in_dim(result_image, wl_index * half, half, 2)
    given = lax.dynamic_slice_in_dim(result_image, (1 - wl_index) * half, half, 2)
    taken = lax.ppermute(given, "wl", perm=[(0, 1), (1, 0)])
    return kept + taken


def solution(mesh):
    in_specs = (P(None, "row", None), P("wl", None, "row", None), P())
    out_specs = P(None, "row", "wl")
    return jax.shard_map(local, mesh=mesh, in_specs=in_specs, out_specs=out_specs, check_vma=False)
```

```python
import math

import jax
import jax.numpy as jnp
from jax import lax
from jax.sharding import PartitionSpec as P

PRECISE = lax.Precision.HIGHEST
NARROW = 32


def phase(left_ids, right_ids, modulus, orient):
    turns = (left_ids * right_ids % modulus).astype(jnp.float32)
    angles = turns * (orient * 2.0 * math.pi / modulus)
    return (jnp.cos(angles), jnp.sin(angles))


def ids(count):
    return jnp.arange(count, dtype=jnp.int32)


def cblock(cos_part, sin_part):
    return jnp.stack([jnp.stack([cos_part, -sin_part]), jnp.stack([sin_part, cos_part])])


def small_tables(out_count, in_count, modulus, orients):
    tables = []
    for orient in orients:
        cos_part, sin_part = phase(ids(out_count)[:, None], ids(in_count)[None, :], modulus, orient)
        tables.append(cblock(cos_part, sin_part))
    return jnp.stack(tables)


def twist(values, axis_e, cos_part, sin_part):
    real = jnp.take(values, 0, axis=axis_e)
    imag = jnp.take(values, 1, axis=axis_e)
    return jnp.stack([real * cos_part - imag * sin_part, real * sin_part + imag * cos_part], axis_e)


def canon_to_groups(canon, group_count):
    mcount, span_c = canon.shape[0], canon.shape[-1] // 2
    mid = canon.shape[1:-1]
    if group_count == mcount:
        return canon
    span = mcount * span_c // group_count
    flat = jnp.moveaxis(canon.reshape((mcount,) + mid + (2, span_c)), 0, -2)
    flat = flat.reshape(mid + (2, group_count, span))
    return jnp.moveaxis(flat, -2, 0).reshape((group_count,) + mid + (2 * span,))


def groups_to_canon(grouped, mcount, axis_g):
    group_count = grouped.shape[axis_g]
    if group_count == mcount:
        return grouped
    moved = jnp.moveaxis(grouped, axis_g, 0)
    mid = moved.shape[1:-1]
    span = moved.shape[-1] // 2
    span_c = group_count * span // mcount
    flat = jnp.moveaxis(moved.reshape((group_count,) + mid + (2, span)), 0, -2)
    flat = flat.reshape(mid + (2, mcount, span_c))
    canon = jnp.moveaxis(flat, -2, 0).reshape((mcount,) + mid + (2 * span_c,))
    return jnp.moveaxis(canon, 0, axis_g)


def forward_rows(scenes):
    rows_here, length = scenes.shape[1], scenes.shape[2]
    across = length // NARROW
    half_k = across // 2
    grid = scenes.reshape((2, rows_here, NARROW, across))
    first_tab = jnp.transpose(small_tables(NARROW, NARROW, NARROW, (-1.0, 1.0)), (0, 3, 1, 2, 4))
    first = jnp.einsum("oaedb,drbn->oaern", first_tab, grid, precision=PRECISE)
    tw_cos, tw_sin = [], []
    for orient in (-1.0, 1.0):
        cos_part, sin_part = phase(ids(NARROW)[:, None], ids(across)[None, :], length, orient)
        tw_cos.append(cos_part)
        tw_sin.append(sin_part)
    tw_cos = jnp.stack(tw_cos)[:, :, None, :]
    tw_sin = jnp.stack(tw_sin)[:, :, None, :]
    turned = twist(first, 2, tw_cos, tw_sin)
    second_tab = jnp.transpose(small_tables(half_k, across, across, (-1.0, 1.0)), (0, 2, 4, 1, 3))
    second = jnp.einsum("oaern,oenfk->oarfk", turned, second_tab, precision=PRECISE)
    signs = 1.0 - 2.0 * (ids(across) % 2).astype(jnp.float32)
    nyquist = jnp.einsum("ern,n->er", first[0, 0], signs, precision=PRECISE)
    per_block = across // NARROW
    mcount = half_k // per_block
    blocks = second.reshape((2, NARROW, rows_here, 2, mcount, per_block))
    canon = jnp.transpose(blocks, (4, 3, 2, 0, 5, 1)).reshape((mcount, 2, rows_here, 2 * across))
    canon = canon.at[0, :, :, across].set(nyquist)
    return canon


def forward_cols(columns):
    length, width = columns.shape[1], columns.shape[2]
    across = length // NARROW
    grid = columns.reshape((2, NARROW, across, width))
    first_tab = jnp.transpose(small_tables(NARROW, NARROW, NARROW, (-1.0, 1.0)), (0, 3, 1, 2, 4))
    first = jnp.einsum("oafeb,ebnj->oafnj", first_tab, grid, precision=PRECISE)
    tw_cos, tw_sin = [], []
    for orient in (-1.0, 1.0):
        cos_part, sin_part = phase(ids(NARROW)[:, None], ids(across)[None, :], length, orient)
        tw_cos.append(cos_part)
        tw_sin.append(sin_part)
    tw_cos = jnp.stack(tw_cos)[:, :, :, None]
    tw_sin = jnp.stack(tw_sin)[:, :, :, None]
    turned = twist(first, 2, tw_cos, tw_sin)
    second_tab = small_tables(across, across, across, (-1.0, 1.0))
    second = jnp.einsum("ofekn,oaenj->ofkaj", second_tab, turned, precision=PRECISE)
    return second.reshape((2, 2, length, width))


def inverse_cols(combined):
    length, width = combined.shape[1], combined.shape[2]
    across = length // NARROW
    grid = combined.reshape((2, NARROW, across, width))
    first_tab = jnp.transpose(small_tables(NARROW, NARROW, NARROW, (1.0,))[0], (2, 0, 1, 3))
    first = jnp.einsum("afeb,ebnj->afnj", first_tab, grid, precision=PRECISE)
    cos_part, sin_part = phase(ids(NARROW)[:, None], ids(across)[None, :], length, 1.0)
    turned = twist(first, 1, cos_part[:, :, None], sin_part[:, :, None])
    second_tab = jnp.transpose(small_tables(across, across, across, (1.0,))[0], (0, 2, 1, 3))
    second = jnp.einsum("fken,aenj->fkaj", second_tab, turned, precision=PRECISE)
    return second.reshape((2, length, width))


def inverse_rows(canon, length, scale):
    mcount, rows_here, width = canon.shape[1], canon.shape[2], canon.shape[3]
    across = width // 2
    first_tab = jnp.transpose(small_tables(NARROW, mcount, NARROW, (1.0, -1.0)), (0, 3, 1, 2, 4))
    first = jnp.einsum("oafem,emRj->oafRj", first_tab, canon, precision=PRECISE)
    lower = first[0, :, :, :, :across]
    upper = first[1, :, :, :, across:]
    flip_gain = -2.0 * (ids(NARROW) % 2).astype(jnp.float32)
    fix = flip_gain[:, None, None] * canon[:, 0, :, across][None]
    lane0 = (ids(across) == 0)[None, None, None, :]
    upper = jnp.where(lane0, upper + fix[..., None], upper)
    cos_up, sin_up = phase(ids(NARROW)[:, None], ids(across)[None, :], length, 1.0)
    cos_dn, sin_dn = phase(ids(NARROW)[:, None], ids(across)[None, :], length, -1.0)
    lower = twist(lower, 1, cos_up[:, None, :], sin_up[:, None, :])
    upper = twist(upper, 1, cos_dn[:, None, :], sin_dn[:, None, :])
    tabs = small_tables(across, across, across, (1.0, -1.0)) * scale
    tabs = jnp.transpose(tabs, (0, 2, 4, 1, 3))
    out = jnp.einsum("aeRu,eufk->aRfk", lower, tabs[0], precision=PRECISE)
    out = out + jnp.einsum("aeRu,eufk->aRfk", upper, tabs[1], precision=PRECISE)
    return jnp.transpose(out, (2, 1, 3, 0)).reshape((2, rows_here, length))


def pair_optics(optics):
    length = optics.shape[-1]
    across = length // NARROW
    half = length // 2
    mcount = half // across
    block = [lax.slice_in_dim(optics, across * i, across * (i + 1), axis=3) for i in range(NARROW)]
    windows = []
    for m in range(mcount):
        second = block[(half // across) if m == 0 else (NARROW - m)]
        windows.append(jnp.concatenate([block[NARROW - 1 - m], second], -1))
    windows = jnp.stack(windows)
    src = ids(2 * across)[:, None]
    dst = ids(across)[None, :]
    picker = jnp.logical_or(
        jnp.logical_and(src == across - dst, dst > 0), jnp.logical_and(src == across, dst == 0)
    ).astype(optics.dtype)
    mirrored = jnp.einsum("mwcpv,vu->mwcpu", windows, picker, preferred_element_type=jnp.float32)
    lower = jnp.stack(block[:mcount])
    return jnp.concatenate([lower, mirrored.astype(optics.dtype)], -1)


def local(scenes, optics, weights):
    row_count = lax.axis_size("row")
    length = scenes.shape[2]
    across = length // NARROW
    norm_factor = 1.0 / (float(length) * float(length))
    wl_index = lax.axis_index("wl")
    local_waves = optics.shape[0]
    weight_rows = lax.dynamic_slice_in_dim(weights, wl_index * local_waves, local_waves, 0)
    first_row = lax.axis_index("row") == 0

    wl_count = lax.axis_size("wl")
    rows_here = scenes.shape[1]
    own_rows = rows_here // wl_count
    if wl_count == 2 and own_rows * wl_count == rows_here:
        mine = lax.dynamic_slice_in_dim(scenes, wl_index * own_rows, own_rows, 1)
        canon = forward_rows(mine)
        mcount = canon.shape[0]
        sent = canon_to_groups(canon, row_count)
        got = lax.all_to_all(sent, "row", split_axis=0, concat_axis=2, tiled=True)[0]
        other = lax.ppermute(got, "wl", perm=[(0, 1), (1, 0)])
        got = got.reshape((2, row_count, own_rows, got.shape[-1]))
        other = other.reshape(got.shape)
        first_half = jnp.where(wl_index == 0, got, other)
        second_half = jnp.where(wl_index == 0, other, got)
        got = jnp.stack([first_half, second_half], 2).reshape((2, length, got.shape[-1]))
    else:
        canon = forward_rows(scenes)
        mcount = canon.shape[0]
        sent = canon_to_groups(canon, row_count)
        got = lax.all_to_all(sent, "row", split_axis=0, concat_axis=2, tiled=True)[0]
    spec = forward_cols(got)

    optic_canon = pair_optics(optics)
    optic_sent = canon_to_groups(optic_canon, row_count)
    optic_got = lax.all_to_all(optic_sent, "row", split_axis=0, concat_axis=3, tiled=True)[0]

    width = spec.shape[-1]
    span = width // 2
    lane_ids = ids(width)
    itself = jnp.logical_and(first_row, lane_ids % span == 0)
    direct = spec[0]
    flipped = spec[1]
    swapped = jnp.concatenate([flipped[..., span:], flipped[..., :span]], -1)
    partner = jnp.where(itself, flipped, swapped)
    mirror_real = partner[0]
    mirror_imag = -partner[1]
    even_real = 0.5 * (direct[0] + mirror_real)
    even_imag = 0.5 * (direct[1] + mirror_imag)
    odd_real = 0.5 * (direct[0] - mirror_real)
    odd_imag = 0.5 * (direct[1] - mirror_imag)
    combined_real = jnp.zeros_like(even_real)
    combined_imag = jnp.zeros_like(even_imag)
    for colour in range(local_waves):
        mixed_real = weight_rows[colour, 0] * even_real + weight_rows[colour, 1] * odd_real
        mixed_imag = weight_rows[colour, 0] * even_imag + weight_rows[colour, 1] * odd_imag
        resp_real = optic_got[colour, 0].astype(jnp.float32)
        resp_imag = optic_got[colour, 1].astype(jnp.float32)
        combined_real = combined_real + resp_real * mixed_real - resp_imag * mixed_imag
        combined_imag = combined_imag + resp_real * mixed_imag + resp_imag * mixed_real

    back = inverse_cols(jnp.stack([combined_real, combined_imag]))
    back = back.reshape((2, row_count, rows_here, width))
    returned = lax.all_to_all(back, "row", split_axis=1, concat_axis=1, tiled=True)
    returned = groups_to_canon(returned, mcount, 1)
    result_image = inverse_rows(returned, length, norm_factor)
    if wl_count != 2:
        return lax.psum_scatter(result_image, "wl", scatter_dimension=2, tiled=True)
    half = length // 2
    kept = lax.dynamic_slice_in_dim(result_image, wl_index * half, half, 2)
    given = lax.dynamic_slice_in_dim(result_image, (1 - wl_index) * half, half, 2)
    taken = lax.ppermute(given, "wl", perm=[(0, 1), (1, 0)])
    return kept + taken


def solution(mesh):
    in_specs = (P(None, "row", None), P("wl", None, "row", None), P())
    out_specs = P(None, "row", "wl")
    return jax.shard_map(local, mesh=mesh, in_specs=in_specs, out_specs=out_specs, check_vma=False)
```

```python
import math

import jax
import jax.numpy as jnp
from jax import lax
from jax.sharding import PartitionSpec as P

PRECISE = lax.Precision.HIGHEST
NARROW = 32


def phase(left_ids, right_ids, modulus, orient):
    turns = (left_ids * right_ids % modulus).astype(jnp.float32)
    angles = turns * (orient * 2.0 * math.pi / modulus)
    return (jnp.cos(angles), jnp.sin(angles))


def ids(count):
    return jnp.arange(count, dtype=jnp.int32)


def cblock(cos_part, sin_part):
    return jnp.stack([jnp.stack([cos_part, -sin_part]), jnp.stack([sin_part, cos_part])])


def small_tables(out_count, in_count, modulus, orients):
    tables = []
    for orient in orients:
        cos_part, sin_part = phase(ids(out_count)[:, None], ids(in_count)[None, :], modulus, orient)
        tables.append(cblock(cos_part, sin_part))
    return jnp.stack(tables)


def twist(values, axis_e, cos_part, sin_part):
    real = jnp.take(values, 0, axis=axis_e)
    imag = jnp.take(values, 1, axis=axis_e)
    return jnp.stack([real * cos_part - imag * sin_part, real * sin_part + imag * cos_part], axis_e)


def canon_to_groups(canon, group_count):
    mcount, span_c = canon.shape[0], canon.shape[-1] // 2
    mid = canon.shape[1:-1]
    if group_count == mcount:
        return canon
    span = mcount * span_c // group_count
    flat = jnp.moveaxis(canon.reshape((mcount,) + mid + (2, span_c)), 0, -2)
    flat = flat.reshape(mid + (2, group_count, span))
    return jnp.moveaxis(flat, -2, 0).reshape((group_count,) + mid + (2 * span,))


def groups_to_canon(grouped, mcount, axis_g):
    group_count = grouped.shape[axis_g]
    if group_count == mcount:
        return grouped
    moved = jnp.moveaxis(grouped, axis_g, 0)
    mid = moved.shape[1:-1]
    span = moved.shape[-1] // 2
    span_c = group_count * span // mcount
    flat = jnp.moveaxis(moved.reshape((group_count,) + mid + (2, span)), 0, -2)
    flat = flat.reshape(mid + (2, mcount, span_c))
    canon = jnp.moveaxis(flat, -2, 0).reshape((mcount,) + mid + (2 * span_c,))
    return jnp.moveaxis(canon, 0, axis_g)


def forward_rows(scenes):
    rows_here, length = scenes.shape[1], scenes.shape[2]
    across = length // NARROW
    half_k = across // 2
    grid = scenes.reshape((2, rows_here, NARROW, across))
    first_tab = jnp.transpose(small_tables(NARROW, NARROW, NARROW, (-1.0, 1.0)), (0, 3, 1, 2, 4))
    first = jnp.einsum("oaedb,drbn->oaern", first_tab, grid, precision=PRECISE)
    tw_cos, tw_sin = [], []
    for orient in (-1.0, 1.0):
        cos_part, sin_part = phase(ids(NARROW)[:, None], ids(across)[None, :], length, orient)
        tw_cos.append(cos_part)
        tw_sin.append(sin_part)
    tw_cos = jnp.stack(tw_cos)[:, :, None, :]
    tw_sin = jnp.stack(tw_sin)[:, :, None, :]
    turned = twist(first, 2, tw_cos, tw_sin)
    second_tab = jnp.transpose(small_tables(half_k, across, across, (-1.0, 1.0)), (0, 2, 4, 1, 3))
    second = jnp.einsum("oaern,oenfk->oarfk", turned, second_tab, precision=PRECISE)
    signs = 1.0 - 2.0 * (ids(across) % 2).astype(jnp.float32)
    nyquist = jnp.einsum("ern,n->er", first[0, 0], signs, precision=PRECISE)
    per_block = across // NARROW
    mcount = half_k // per_block
    blocks = second.reshape((2, NARROW, rows_here, 2, mcount, per_block))
    canon = jnp.transpose(blocks, (4, 3, 2, 0, 5, 1)).reshape((mcount, 2, rows_here, 2 * across))
    canon = canon.at[0, :, :, across].set(nyquist)
    return canon


def forward_cols(columns):
    length, width = columns.shape[1], columns.shape[2]
    across = length // NARROW
    grid = columns.reshape((2, NARROW, across, width))
    first_tab = jnp.transpose(small_tables(NARROW, NARROW, NARROW, (-1.0, 1.0)), (0, 3, 1, 2, 4))
    first = jnp.einsum("oafeb,ebnj->oafnj", first_tab, grid, precision=PRECISE)
    tw_cos, tw_sin = [], []
    for orient in (-1.0, 1.0):
        cos_part, sin_part = phase(ids(NARROW)[:, None], ids(across)[None, :], length, orient)
        tw_cos.append(cos_part)
        tw_sin.append(sin_part)
    tw_cos = jnp.stack(tw_cos)[:, :, :, None]
    tw_sin = jnp.stack(tw_sin)[:, :, :, None]
    turned = twist(first, 2, tw_cos, tw_sin)
    second_tab = small_tables(across, across, across, (-1.0, 1.0))
    second = jnp.einsum("ofekn,oaenj->ofkaj", second_tab, turned, precision=PRECISE)
    return second.reshape((2, 2, length, width))


def inverse_cols(combined):
    length, width = combined.shape[1], combined.shape[2]
    across = length // NARROW
    grid = combined.reshape((2, NARROW, across, width))
    first_tab = jnp.transpose(small_tables(NARROW, NARROW, NARROW, (1.0,))[0], (2, 0, 1, 3))
    first = jnp.einsum("afeb,ebnj->afnj", first_tab, grid, precision=PRECISE)
    cos_part, sin_part = phase(ids(NARROW)[:, None], ids(across)[None, :], length, 1.0)
    turned = twist(first, 1, cos_part[:, :, None], sin_part[:, :, None])
    second_tab = jnp.transpose(small_tables(across, across, across, (1.0,))[0], (0, 2, 1, 3))
    second = jnp.einsum("fken,aenj->fkaj", second_tab, turned, precision=PRECISE)
    return second.reshape((2, length, width))


def inverse_rows(canon, length, scale):
    mcount, rows_here, width = canon.shape[1], canon.shape[2], canon.shape[3]
    across = width // 2
    first_tab = jnp.transpose(small_tables(NARROW, mcount, NARROW, (1.0, -1.0)), (0, 3, 1, 2, 4))
    first = jnp.einsum("oafem,emRj->oafRj", first_tab, canon, precision=PRECISE)
    lower = first[0, :, :, :, :across]
    upper = first[1, :, :, :, across:]
    flip_gain = -2.0 * (ids(NARROW) % 2).astype(jnp.float32)
    fix = flip_gain[:, None, None] * canon[:, 0, :, across][None]
    lane0 = (ids(across) == 0)[None, None, None, :]
    upper = jnp.where(lane0, upper + fix[..., None], upper)
    cos_up, sin_up = phase(ids(NARROW)[:, None], ids(across)[None, :], length, 1.0)
    cos_dn, sin_dn = phase(ids(NARROW)[:, None], ids(across)[None, :], length, -1.0)
    lower = twist(lower, 1, cos_up[:, None, :], sin_up[:, None, :])
    upper = twist(upper, 1, cos_dn[:, None, :], sin_dn[:, None, :])
    tabs = small_tables(across, across, across, (1.0, -1.0)) * scale
    tabs = jnp.transpose(tabs, (0, 2, 4, 1, 3))
    out = jnp.einsum("aeRu,eufk->aRfk", lower, tabs[0], precision=PRECISE)
    out = out + jnp.einsum("aeRu,eufk->aRfk", upper, tabs[1], precision=PRECISE)
    return jnp.transpose(out, (2, 1, 3, 0)).reshape((2, rows_here, length))


def pair_optics(optics):
    length = optics.shape[-1]
    across = length // NARROW
    half = length // 2
    mcount = half // across
    block = [lax.slice_in_dim(optics, across * i, across * (i + 1), axis=3) for i in range(NARROW)]
    windows = []
    for m in range(mcount):
        second = block[(half // across) if m == 0 else (NARROW - m)]
        windows.append(jnp.concatenate([block[NARROW - 1 - m], second], -1))
    windows = jnp.stack(windows)
    src = ids(2 * across)[:, None]
    dst = ids(across)[None, :]
    picker = jnp.logical_or(
        jnp.logical_and(src == across - dst, dst > 0), jnp.logical_and(src == across, dst == 0)
    ).astype(optics.dtype)
    mirrored = jnp.einsum("mwcpv,vu->mwcpu", windows, picker, preferred_element_type=jnp.float32)
    lower = jnp.stack(block[:mcount])
    return jnp.concatenate([lower, mirrored.astype(optics.dtype)], -1)


def local(scenes, optics, weights):
    row_count = lax.axis_size("row")
    length = scenes.shape[2]
    across = length // NARROW
    norm_factor = 1.0 / (float(length) * float(length))
    wl_index = lax.axis_index("wl")
    local_waves = optics.shape[0]
    weight_rows = lax.dynamic_slice_in_dim(weights, wl_index * local_waves, local_waves, 0)
    first_row = lax.axis_index("row") == 0

    wl_count = lax.axis_size("wl")
    rows_here = scenes.shape[1]
    own_rows = rows_here // wl_count
    if wl_count == 2 and own_rows * wl_count == rows_here:
        mine = lax.dynamic_slice_in_dim(scenes, wl_index * own_rows, own_rows, 1)
        canon = forward_rows(mine)
        mcount = canon.shape[0]
        sent = canon_to_groups(canon, row_count)
        got = lax.all_to_all(sent, "row", split_axis=0, concat_axis=2, tiled=True)[0]
        other = lax.ppermute(got, "wl", perm=[(0, 1), (1, 0)])
        got = got.reshape((2, row_count, own_rows, got.shape[-1]))
        other = other.reshape(got.shape)
        first_half = jnp.where(wl_index == 0, got, other)
        second_half = jnp.where(wl_index == 0, other, got)
        got = jnp.stack([first_half, second_half], 2).reshape((2, length, got.shape[-1]))
    else:
        canon = forward_rows(scenes)
        mcount = canon.shape[0]
        sent = canon_to_groups(canon, row_count)
        got = lax.all_to_all(sent, "row", split_axis=0, concat_axis=2, tiled=True)[0]
    spec = forward_cols(got)

    optic_canon = pair_optics(optics)
    optic_sent = canon_to_groups(optic_canon, row_count)
    optic_got = lax.all_to_all(optic_sent, "row", split_axis=0, concat_axis=3, tiled=True)[0]

    width = spec.shape[-1]
    span = width // 2
    lane_ids = ids(width)
    itself = jnp.logical_and(first_row, lane_ids % span == 0)
    direct = spec[0]
    flipped = spec[1]
    swapped = jnp.concatenate([flipped[..., span:], flipped[..., :span]], -1)
    partner = jnp.where(itself, flipped, swapped)
    mirror_real = partner[0]
    mirror_imag = -partner[1]
    even_real = 0.5 * (direct[0] + mirror_real)
    even_imag = 0.5 * (direct[1] + mirror_imag)
    odd_real = 0.5 * (direct[0] - mirror_real)
    odd_imag = 0.5 * (direct[1] - mirror_imag)
    combined_real = jnp.zeros_like(even_real)
    combined_imag = jnp.zeros_like(even_imag)
    for colour in range(local_waves):
        mixed_real = weight_rows[colour, 0] * even_real + weight_rows[colour, 1] * odd_real
        mixed_imag = weight_rows[colour, 0] * even_imag + weight_rows[colour, 1] * odd_imag
        resp_real = optic_got[colour, 0].astype(jnp.float32)
        resp_imag = optic_got[colour, 1].astype(jnp.float32)
        combined_real = combined_real + resp_real * mixed_real - resp_imag * mixed_imag
        combined_imag = combined_imag + resp_real * mixed_imag + resp_imag * mixed_real

    back = inverse_cols(jnp.stack([combined_real, combined_imag]))
    if wl_count != 2 or own_rows * wl_count != rows_here:
        back = back.reshape((2, row_count, rows_here, width))
        returned = lax.all_to_all(back, "row", split_axis=1, concat_axis=1, tiled=True)
        returned = groups_to_canon(returned, mcount, 1)
        result_image = inverse_rows(returned, length, norm_factor)
        return lax.psum_scatter(result_image, "wl", scatter_dimension=2, tiled=True)
    back = back.reshape((2, row_count, 2, own_rows, width))
    kept = lax.dynamic_index_in_dim(back, wl_index, 2, keepdims=False)
    given = lax.dynamic_index_in_dim(back, 1 - wl_index, 2, keepdims=False)
    summed = kept + lax.ppermute(given, "wl", perm=[(0, 1), (1, 0)])
    returned = lax.all_to_all(summed, "row", split_axis=1, concat_axis=1, tiled=True)
    returned = groups_to_canon(returned, mcount, 1)
    result_image = inverse_rows(returned, length, norm_factor)
    half = length // 2
    result_image = result_image.reshape((2, own_rows, 2, half))
    mine = lax.dynamic_index_in_dim(result_image, wl_index, 2, keepdims=False)
    theirs = lax.dynamic_index_in_dim(result_image, 1 - wl_index, 2, keepdims=False)
    taken = lax.ppermute(theirs, "wl", perm=[(0, 1), (1, 0)])
    upper = jnp.where(wl_index == 0, mine, taken)
    lower = jnp.where(wl_index == 0, taken, mine)
    return jnp.concatenate([upper, lower], 1)


def solution(mesh):
    in_specs = (P(None, "row", None), P("wl", None, "row", None), P())
    out_specs = P(None, "row", "wl")
    return jax.shard_map(local, mesh=mesh, in_specs=in_specs, out_specs=out_specs, check_vma=False)
```

```python
import math

import jax
import jax.numpy as jnp
from jax import lax
from jax.sharding import PartitionSpec as P

PRECISE = lax.Precision.HIGHEST
NARROW = 32


def phase(left_ids, right_ids, modulus, orient):
    turns = (left_ids * right_ids % modulus).astype(jnp.float32)
    angles = turns * (orient * 2.0 * math.pi / modulus)
    return (jnp.cos(angles), jnp.sin(angles))


def ids(count):
    return jnp.arange(count, dtype=jnp.int32)


def cblock(cos_part, sin_part):
    return jnp.stack([jnp.stack([cos_part, -sin_part]), jnp.stack([sin_part, cos_part])])


def small_tables(out_count, in_count, modulus, orients):
    tables = []
    for orient in orients:
        cos_part, sin_part = phase(ids(out_count)[:, None], ids(in_count)[None, :], modulus, orient)
        tables.append(cblock(cos_part, sin_part))
    return jnp.stack(tables)


def twist(values, axis_e, cos_part, sin_part):
    real = jnp.take(values, 0, axis=axis_e)
    imag = jnp.take(values, 1, axis=axis_e)
    return jnp.stack([real * cos_part - imag * sin_part, real * sin_part + imag * cos_part], axis_e)


def canon_to_groups(canon, group_count):
    mcount, span_c = canon.shape[0], canon.shape[-1] // 2
    mid = canon.shape[1:-1]
    if group_count == mcount:
        return canon
    span = mcount * span_c // group_count
    flat = jnp.moveaxis(canon.reshape((mcount,) + mid + (2, span_c)), 0, -2)
    flat = flat.reshape(mid + (2, group_count, span))
    return jnp.moveaxis(flat, -2, 0).reshape((group_count,) + mid + (2 * span,))


def groups_to_canon(grouped, mcount, axis_g):
    group_count = grouped.shape[axis_g]
    if group_count == mcount:
        return grouped
    moved = jnp.moveaxis(grouped, axis_g, 0)
    mid = moved.shape[1:-1]
    span = moved.shape[-1] // 2
    span_c = group_count * span // mcount
    flat = jnp.moveaxis(moved.reshape((group_count,) + mid + (2, span)), 0, -2)
    flat = flat.reshape(mid + (2, mcount, span_c))
    canon = jnp.moveaxis(flat, -2, 0).reshape((mcount,) + mid + (2 * span_c,))
    return jnp.moveaxis(canon, 0, axis_g)


def forward_rows(scenes):
    rows_here, length = scenes.shape[1], scenes.shape[2]
    across = length // NARROW
    half_k = across // 2
    grid = scenes.reshape((2, rows_here, NARROW, across))
    first_tab = jnp.transpose(small_tables(NARROW, NARROW, NARROW, (-1.0, 1.0)), (0, 3, 1, 2, 4))
    first = jnp.einsum("oaedb,drbn->oaern", first_tab, grid, precision=PRECISE)
    tw_cos, tw_sin = [], []
    for orient in (-1.0, 1.0):
        cos_part, sin_part = phase(ids(NARROW)[:, None], ids(across)[None, :], length, orient)
        tw_cos.append(cos_part)
        tw_sin.append(sin_part)
    tw_cos = jnp.stack(tw_cos)[:, :, None, :]
    tw_sin = jnp.stack(tw_sin)[:, :, None, :]
    turned = twist(first, 2, tw_cos, tw_sin)
    second_tab = jnp.transpose(small_tables(half_k, across, across, (-1.0, 1.0)), (0, 2, 4, 1, 3))
    second = jnp.einsum("oaern,oenfk->oarfk", turned, second_tab, precision=PRECISE)
    signs = 1.0 - 2.0 * (ids(across) % 2).astype(jnp.float32)
    nyquist = jnp.einsum("ern,n->er", first[0, 0], signs, precision=PRECISE)
    per_block = across // NARROW
    mcount = half_k // per_block
    blocks = second.reshape((2, NARROW, rows_here, 2, mcount, per_block))
    canon = jnp.transpose(blocks, (4, 3, 2, 0, 5, 1)).reshape((mcount, 2, rows_here, 2 * across))
    canon = canon.at[0, :, :, across].set(nyquist)
    return canon


def forward_cols(columns):
    length, width = columns.shape[1], columns.shape[2]
    across = length // NARROW
    grid = columns.reshape((2, NARROW, across, width))
    first_tab = jnp.transpose(small_tables(NARROW, NARROW, NARROW, (-1.0, 1.0)), (0, 3, 1, 2, 4))
    first = jnp.einsum("oafeb,ebnj->oafnj", first_tab, grid, precision=PRECISE)
    tw_cos, tw_sin = [], []
    for orient in (-1.0, 1.0):
        cos_part, sin_part = phase(ids(NARROW)[:, None], ids(across)[None, :], length, orient)
        tw_cos.append(cos_part)
        tw_sin.append(sin_part)
    tw_cos = jnp.stack(tw_cos)[:, :, :, None]
    tw_sin = jnp.stack(tw_sin)[:, :, :, None]
    turned = twist(first, 2, tw_cos, tw_sin)
    second_tab = small_tables(across, across, across, (-1.0, 1.0))
    second = jnp.einsum("ofekn,oaenj->ofkaj", second_tab, turned, precision=PRECISE)
    return second.reshape((2, 2, length, width))


def inverse_cols(combined):
    length, width = combined.shape[1], combined.shape[2]
    across = length // NARROW
    grid = combined.reshape((2, NARROW, across, width))
    first_tab = jnp.transpose(small_tables(NARROW, NARROW, NARROW, (1.0,))[0], (2, 0, 1, 3))
    first = jnp.einsum("afeb,ebnj->afnj", first_tab, grid, precision=PRECISE)
    cos_part, sin_part = phase(ids(NARROW)[:, None], ids(across)[None, :], length, 1.0)
    turned = twist(first, 1, cos_part[:, :, None], sin_part[:, :, None])
    second_tab = jnp.transpose(small_tables(across, across, across, (1.0,))[0], (0, 2, 1, 3))
    second = jnp.einsum("fken,aenj->fkaj", second_tab, turned, precision=PRECISE)
    return second.reshape((2, length, width))


def inverse_rows(canon, length, scale, k_count=None, k_start=0):
    mcount, rows_here, width = canon.shape[1], canon.shape[2], canon.shape[3]
    across = width // 2
    k_count = across if k_count is None else k_count
    first_tab = jnp.transpose(small_tables(NARROW, mcount, NARROW, (1.0, -1.0)), (0, 3, 1, 2, 4))
    first = jnp.einsum("oafem,emRj->oafRj", first_tab, canon, precision=PRECISE)
    lower = first[0, :, :, :, :across]
    upper = first[1, :, :, :, across:]
    flip_gain = -2.0 * (ids(NARROW) % 2).astype(jnp.float32)
    fix = flip_gain[:, None, None] * canon[:, 0, :, across][None]
    lane0 = (ids(across) == 0)[None, None, None, :]
    upper = jnp.where(lane0, upper + fix[..., None], upper)
    cos_up, sin_up = phase(ids(NARROW)[:, None], ids(across)[None, :], length, 1.0)
    cos_dn, sin_dn = phase(ids(NARROW)[:, None], ids(across)[None, :], length, -1.0)
    lower = twist(lower, 1, cos_up[:, None, :], sin_up[:, None, :])
    upper = twist(upper, 1, cos_dn[:, None, :], sin_dn[:, None, :])
    tabs = []
    for orient in (1.0, -1.0):
        k_ids = ids(k_count)[:, None] + k_start
        cos_part, sin_part = phase(k_ids, ids(across)[None, :], across, orient)
        tabs.append(cblock(cos_part, sin_part))
    tabs = jnp.transpose(jnp.stack(tabs) * scale, (0, 2, 4, 1, 3))
    out = jnp.einsum("aeRu,eufk->aRfk", lower, tabs[0], precision=PRECISE)
    out = out + jnp.einsum("aeRu,eufk->aRfk", upper, tabs[1], precision=PRECISE)
    return jnp.transpose(out, (2, 1, 3, 0)).reshape((2, rows_here, k_count * NARROW))


def pair_optics(optics):
    length = optics.shape[-1]
    across = length // NARROW
    half = length // 2
    mcount = half // across
    block = [lax.slice_in_dim(optics, across * i, across * (i + 1), axis=3) for i in range(NARROW)]
    windows = []
    for m in range(mcount):
        second = block[(half // across) if m == 0 else (NARROW - m)]
        windows.append(jnp.concatenate([block[NARROW - 1 - m], second], -1))
    windows = jnp.stack(windows)
    src = ids(2 * across)[:, None]
    dst = ids(across)[None, :]
    picker = jnp.logical_or(
        jnp.logical_and(src == across - dst, dst > 0), jnp.logical_and(src == across, dst == 0)
    ).astype(optics.dtype)
    mirrored = jnp.einsum("mwcpv,vu->mwcpu", windows, picker, preferred_element_type=jnp.float32)
    lower = jnp.stack(block[:mcount])
    return jnp.concatenate([lower, mirrored.astype(optics.dtype)], -1)


def split_lanes(grouped, half_index):
    span = grouped.shape[-1] // 2
    lead = grouped.shape[:-1]
    parts = grouped.reshape(lead + (2, 2, span // 2))
    picked = lax.dynamic_index_in_dim(parts, half_index, len(lead) + 1, keepdims=False)
    return picked.reshape(lead + (span,))


def join_lanes(mine, theirs, half_index):
    lead = mine.shape[:-1]
    quarter = mine.shape[-1] // 2
    mine = mine.reshape(lead + (2, quarter))
    theirs = theirs.reshape(lead + (2, quarter))
    low = jnp.where(half_index == 0, mine, theirs)
    high = jnp.where(half_index == 0, theirs, mine)
    return jnp.stack([low, high], -2).reshape(lead + (4 * quarter,))


def combine(spec, optic_got, weight_rows, itself):
    width = spec.shape[-1]
    span = width // 2
    direct = spec[0]
    flipped = spec[1]
    swapped = jnp.concatenate([flipped[..., span:], flipped[..., :span]], -1)
    partner = jnp.where(itself, flipped, swapped)
    mirror_real = partner[0]
    mirror_imag = -partner[1]
    even_real = 0.5 * (direct[0] + mirror_real)
    even_imag = 0.5 * (direct[1] + mirror_imag)
    odd_real = 0.5 * (direct[0] - mirror_real)
    odd_imag = 0.5 * (direct[1] - mirror_imag)
    combined_real = jnp.zeros_like(even_real)
    combined_imag = jnp.zeros_like(even_imag)
    for colour in range(optic_got.shape[0]):
        mixed_real = weight_rows[colour, 0] * even_real + weight_rows[colour, 1] * odd_real
        mixed_imag = weight_rows[colour, 0] * even_imag + weight_rows[colour, 1] * odd_imag
        resp_real = optic_got[colour, 0].astype(jnp.float32)
        resp_imag = optic_got[colour, 1].astype(jnp.float32)
        combined_real = combined_real + resp_real * mixed_real - resp_imag * mixed_imag
        combined_imag = combined_imag + resp_real * mixed_imag + resp_imag * mixed_real
    return jnp.stack([combined_real, combined_imag])


def local_split(scenes, optics, weights):
    row_count = lax.axis_size("row")
    rows_here, length = scenes.shape[1], scenes.shape[2]
    across = length // NARROW
    norm_factor = 1.0 / (float(length) * float(length))
    wl_index = lax.axis_index("wl")
    first_row = lax.axis_index("row") == 0
    swap = [(0, 1), (1, 0)]

    optic_canon = pair_optics(optics)
    optic_grouped = canon_to_groups(optic_canon, row_count)
    optic_mine = split_lanes(optic_grouped, wl_index)
    optic_theirs = lax.ppermute(split_lanes(optic_grouped, 1 - wl_index), "wl", perm=swap)
    optic_low = jnp.where(wl_index == 0, optic_mine, optic_theirs)
    optic_high = jnp.where(wl_index == 0, optic_theirs, optic_mine)
    optic_all = jnp.concatenate([optic_low, optic_high], 1)
    optic_got = lax.all_to_all(optic_all, "row", split_axis=0, concat_axis=3, tiled=True)[0]

    canon = forward_rows(scenes)
    mcount = canon.shape[0]
    sent = split_lanes(canon_to_groups(canon, row_count), wl_index)
    got = lax.all_to_all(sent, "row", split_axis=0, concat_axis=2, tiled=True)[0]
    spec = forward_cols(got)

    width = spec.shape[-1]
    lane_ids = ids(width)
    itself = jnp.logical_and(first_row, wl_index == 0)
    itself = jnp.logical_and(itself, lane_ids % (width // 2) == 0)
    combined = combine(spec, optic_got, weights, itself)

    back = inverse_cols(combined)
    back = back.reshape((2, row_count, rows_here, width))
    returned = lax.all_to_all(back, "row", split_axis=1, concat_axis=1, tiled=True)
    other = lax.ppermute(returned, "wl", perm=swap)
    returned = join_lanes(returned, other, wl_index)
    returned = groups_to_canon(returned, mcount, 1)
    k_half = across // 2
    return inverse_rows(returned, length, norm_factor, k_half, wl_index * k_half)


def local(scenes, optics, weights):
    row_count = lax.axis_size("row")
    length = scenes.shape[2]
    span = length // 2 // row_count
    if lax.axis_size("wl") == 2 and span % 2 == 0:
        return local_split(scenes, optics, weights)
    norm_factor = 1.0 / (float(length) * float(length))
    wl_index = lax.axis_index("wl")
    local_waves = optics.shape[0]
    weight_rows = lax.dynamic_slice_in_dim(weights, wl_index * local_waves, local_waves, 0)
    first_row = lax.axis_index("row") == 0
    canon = forward_rows(scenes)
    mcount = canon.shape[0]
    sent = canon_to_groups(canon, row_count)
    got = lax.all_to_all(sent, "row", split_axis=0, concat_axis=2, tiled=True)[0]
    spec = forward_cols(got)
    optic_grouped = canon_to_groups(pair_optics(optics), row_count)
    optic_got = lax.all_to_all(optic_grouped, "row", split_axis=0, concat_axis=3, tiled=True)[0]
    width = spec.shape[-1]
    itself = jnp.logical_and(first_row, ids(width) % (width // 2) == 0)
    combined = combine(spec, optic_got, weight_rows, itself)
    back = inverse_cols(combined)
    rows_here = scenes.shape[1]
    back = back.reshape((2, row_count, rows_here, width))
    returned = lax.all_to_all(back, "row", split_axis=1, concat_axis=1, tiled=True)
    returned = groups_to_canon(returned, mcount, 1)
    result_image = inverse_rows(returned, length, norm_factor)
    return lax.psum_scatter(result_image, "wl", scatter_dimension=2, tiled=True)


def solution(mesh):
    in_specs = (P(None, "row", None), P("wl", None, "row", None), P())
    out_specs = P(None, "row", "wl")
    return jax.shard_map(local, mesh=mesh, in_specs=in_specs, out_specs=out_specs, check_vma=False)
```

```python
import math

import jax
import jax.numpy as jnp
from jax import lax
from jax.sharding import PartitionSpec as P

PRECISE = lax.Precision.HIGHEST
NARROW = 32


def phase(left_ids, right_ids, modulus, orient):
    turns = (left_ids * right_ids % modulus).astype(jnp.float32)
    angles = turns * (orient * 2.0 * math.pi / modulus)
    return (jnp.cos(angles), jnp.sin(angles))


def ids(count):
    return jnp.arange(count, dtype=jnp.int32)


def cblock(cos_part, sin_part):
    return jnp.stack([jnp.stack([cos_part, -sin_part]), jnp.stack([sin_part, cos_part])])


def small_tables(out_count, in_count, modulus, orients):
    tables = []
    for orient in orients:
        cos_part, sin_part = phase(ids(out_count)[:, None], ids(in_count)[None, :], modulus, orient)
        tables.append(cblock(cos_part, sin_part))
    return jnp.stack(tables)


def twist(values, axis_e, cos_part, sin_part):
    real = jnp.take(values, 0, axis=axis_e)
    imag = jnp.take(values, 1, axis=axis_e)
    return jnp.stack([real * cos_part - imag * sin_part, real * sin_part + imag * cos_part], axis_e)


def canon_to_groups(canon, group_count):
    mcount, span_c = canon.shape[0], canon.shape[-1] // 2
    mid = canon.shape[1:-1]
    if group_count == mcount:
        return canon
    span = mcount * span_c // group_count
    flat = jnp.moveaxis(canon.reshape((mcount,) + mid + (2, span_c)), 0, -2)
    flat = flat.reshape(mid + (2, group_count, span))
    return jnp.moveaxis(flat, -2, 0).reshape((group_count,) + mid + (2 * span,))


def groups_to_canon(grouped, mcount, axis_g):
    group_count = grouped.shape[axis_g]
    if group_count == mcount:
        return grouped
    moved = jnp.moveaxis(grouped, axis_g, 0)
    mid = moved.shape[1:-1]
    span = moved.shape[-1] // 2
    span_c = group_count * span // mcount
    flat = jnp.moveaxis(moved.reshape((group_count,) + mid + (2, span)), 0, -2)
    flat = flat.reshape(mid + (2, mcount, span_c))
    canon = jnp.moveaxis(flat, -2, 0).reshape((mcount,) + mid + (2 * span_c,))
    return jnp.moveaxis(canon, 0, axis_g)


def forward_rows(scenes):
    rows_here, length = scenes.shape[1], scenes.shape[2]
    across = length // NARROW
    half_k = across // 2
    grid = scenes.reshape((2, rows_here, NARROW, across))
    first_tab = jnp.transpose(small_tables(NARROW, NARROW, NARROW, (-1.0, 1.0)), (0, 3, 1, 2, 4))
    first = jnp.einsum("oaedb,drbn->oaern", first_tab, grid, precision=PRECISE)
    tw_cos, tw_sin = [], []
    for orient in (-1.0, 1.0):
        cos_part, sin_part = phase(ids(NARROW)[:, None], ids(across)[None, :], length, orient)
        tw_cos.append(cos_part)
        tw_sin.append(sin_part)
    tw_cos = jnp.stack(tw_cos)[:, :, None, :]
    tw_sin = jnp.stack(tw_sin)[:, :, None, :]
    turned = twist(first, 2, tw_cos, tw_sin)
    second_tab = jnp.transpose(small_tables(half_k, across, across, (-1.0, 1.0)), (0, 2, 4, 1, 3))
    second = jnp.einsum("oaern,oenfk->oarfk", turned, second_tab, precision=PRECISE)
    signs = 1.0 - 2.0 * (ids(across) % 2).astype(jnp.float32)
    nyquist = jnp.einsum("ern,n->er", first[0, 0], signs, precision=PRECISE)
    per_block = across // NARROW
    mcount = half_k // per_block
    blocks = second.reshape((2, NARROW, rows_here, 2, mcount, per_block))
    canon = jnp.transpose(blocks, (4, 3, 2, 0, 5, 1)).reshape((mcount, 2, rows_here, 2 * across))
    canon = canon.at[0, :, :, across].set(nyquist)
    return canon


def forward_cols(columns):
    length, width = columns.shape[1], columns.shape[2]
    across = length // NARROW
    grid = columns.reshape((2, NARROW, across, width))
    first_tab = jnp.transpose(small_tables(NARROW, NARROW, NARROW, (-1.0, 1.0)), (0, 3, 1, 2, 4))
    first = jnp.einsum("oafeb,ebnj->oafnj", first_tab, grid, precision=PRECISE)
    tw_cos, tw_sin = [], []
    for orient in (-1.0, 1.0):
        cos_part, sin_part = phase(ids(NARROW)[:, None], ids(across)[None, :], length, orient)
        tw_cos.append(cos_part)
        tw_sin.append(sin_part)
    tw_cos = jnp.stack(tw_cos)[:, :, :, None]
    tw_sin = jnp.stack(tw_sin)[:, :, :, None]
    turned = twist(first, 2, tw_cos, tw_sin)
    second_tab = small_tables(across, across, across, (-1.0, 1.0))
    second = jnp.einsum("ofekn,oaenj->ofkaj", second_tab, turned, precision=PRECISE)
    return second.reshape((2, 2, length, width))


def inverse_cols(combined):
    length, width = combined.shape[1], combined.shape[2]
    across = length // NARROW
    grid = combined.reshape((2, NARROW, across, width))
    first_tab = jnp.transpose(small_tables(NARROW, NARROW, NARROW, (1.0,))[0], (2, 0, 1, 3))
    first = jnp.einsum("afeb,ebnj->afnj", first_tab, grid, precision=PRECISE)
    cos_part, sin_part = phase(ids(NARROW)[:, None], ids(across)[None, :], length, 1.0)
    turned = twist(first, 1, cos_part[:, :, None], sin_part[:, :, None])
    second_tab = jnp.transpose(small_tables(across, across, across, (1.0,))[0], (0, 2, 1, 3))
    second = jnp.einsum("fken,aenj->fkaj", second_tab, turned, precision=PRECISE)
    return second.reshape((2, length, width))


def inverse_rows(canon, length, scale, k_count=None, k_start=0):
    mcount, rows_here, width = canon.shape[1], canon.shape[2], canon.shape[3]
    across = width // 2
    k_count = across if k_count is None else k_count
    first_tab = jnp.transpose(small_tables(NARROW, mcount, NARROW, (1.0, -1.0)), (0, 3, 1, 2, 4))
    first = jnp.einsum("oafem,emRj->oafRj", first_tab, canon, precision=PRECISE)
    lower = first[0, :, :, :, :across]
    upper = first[1, :, :, :, across:]
    flip_gain = -2.0 * (ids(NARROW) % 2).astype(jnp.float32)
    fix = flip_gain[:, None, None] * canon[:, 0, :, across][None]
    lane0 = (ids(across) == 0)[None, None, None, :]
    upper = jnp.where(lane0, upper + fix[..., None], upper)
    cos_up, sin_up = phase(ids(NARROW)[:, None], ids(across)[None, :], length, 1.0)
    cos_dn, sin_dn = phase(ids(NARROW)[:, None], ids(across)[None, :], length, -1.0)
    lower = twist(lower, 1, cos_up[:, None, :], sin_up[:, None, :])
    upper = twist(upper, 1, cos_dn[:, None, :], sin_dn[:, None, :])
    tabs = []
    for orient in (1.0, -1.0):
        k_ids = ids(k_count)[:, None] + k_start
        cos_part, sin_part = phase(k_ids, ids(across)[None, :], across, orient)
        tabs.append(cblock(cos_part, sin_part))
    tabs = jnp.transpose(jnp.stack(tabs) * scale, (0, 2, 4, 1, 3))
    out = jnp.einsum("aeRu,eufk->aRfk", lower, tabs[0], precision=PRECISE)
    out = out + jnp.einsum("aeRu,eufk->aRfk", upper, tabs[1], precision=PRECISE)
    return jnp.transpose(out, (2, 1, 3, 0)).reshape((2, rows_here, k_count * NARROW))


def pair_optics(optics):
    length = optics.shape[-1]
    across = length // NARROW
    half = length // 2
    mcount = half // across
    block = [lax.slice_in_dim(optics, across * i, across * (i + 1), axis=3) for i in range(NARROW)]
    windows = []
    for m in range(mcount):
        second = block[(half // across) if m == 0 else (NARROW - m)]
        windows.append(jnp.concatenate([block[NARROW - 1 - m], second], -1))
    windows = jnp.stack(windows)
    src = ids(2 * across)[:, None]
    dst = ids(across)[None, :]
    picker = jnp.logical_or(
        jnp.logical_and(src == across - dst, dst > 0), jnp.logical_and(src == across, dst == 0)
    ).astype(optics.dtype)
    mirrored = jnp.einsum("mwcpv,vu->mwcpu", windows, picker, preferred_element_type=jnp.float32)
    lower = jnp.stack(block[:mcount])
    return jnp.concatenate([lower, mirrored.astype(optics.dtype)], -1)


def split_lanes(grouped, half_index):
    span = grouped.shape[-1] // 2
    lead = grouped.shape[:-1]
    parts = grouped.reshape(lead + (2, 2, span // 2))
    picked = lax.dynamic_index_in_dim(parts, half_index, len(lead) + 1, keepdims=False)
    return picked.reshape(lead + (span,))


def join_lanes(mine, theirs, half_index):
    lead = mine.shape[:-1]
    quarter = mine.shape[-1] // 2
    mine = mine.reshape(lead + (2, quarter))
    theirs = theirs.reshape(lead + (2, quarter))
    low = jnp.where(half_index == 0, mine, theirs)
    high = jnp.where(half_index == 0, theirs, mine)
    return jnp.stack([low, high], -2).reshape(lead + (4 * quarter,))


def combine(spec, optic_got, weight_rows, itself):
    width = spec.shape[-1]
    span = width // 2
    direct = spec[0]
    flipped = spec[1]
    swapped = jnp.concatenate([flipped[..., span:], flipped[..., :span]], -1)
    partner = jnp.where(itself, flipped, swapped)
    mirror_real = partner[0]
    mirror_imag = -partner[1]
    even_real = 0.5 * (direct[0] + mirror_real)
    even_imag = 0.5 * (direct[1] + mirror_imag)
    odd_real = 0.5 * (direct[0] - mirror_real)
    odd_imag = 0.5 * (direct[1] - mirror_imag)
    combined_real = jnp.zeros_like(even_real)
    combined_imag = jnp.zeros_like(even_imag)
    for colour in range(optic_got.shape[0]):
        mixed_real = weight_rows[colour, 0] * even_real + weight_rows[colour, 1] * odd_real
        mixed_imag = weight_rows[colour, 0] * even_imag + weight_rows[colour, 1] * odd_imag
        resp_real = optic_got[colour, 0].astype(jnp.float32)
        resp_imag = optic_got[colour, 1].astype(jnp.float32)
        combined_real = combined_real + resp_real * mixed_real - resp_imag * mixed_imag
        combined_imag = combined_imag + resp_real * mixed_imag + resp_imag * mixed_real
    return jnp.stack([combined_real, combined_imag])


def local_split(scenes, optics, weights):
    row_count = lax.axis_size("row")
    rows_here, length = scenes.shape[1], scenes.shape[2]
    across = length // NARROW
    norm_factor = 1.0 / (float(length) * float(length))
    wl_index = lax.axis_index("wl")
    first_row = lax.axis_index("row") == 0
    swap = [(0, 1), (1, 0)]

    optic_grouped = canon_to_groups(pair_optics(optics), row_count)
    optic_own = lax.all_to_all(optic_grouped, "row", split_axis=0, concat_axis=3, tiled=True)[0]

    canon = forward_rows(scenes)
    mcount = canon.shape[0]
    sent = split_lanes(canon_to_groups(canon, row_count), wl_index)
    optic_own, sent = lax.optimization_barrier((optic_own, sent))
    got = lax.all_to_all(sent, "row", split_axis=0, concat_axis=2, tiled=True)[0]
    optic_mine = split_lanes(optic_own, wl_index)
    optic_theirs = lax.ppermute(split_lanes(optic_own, 1 - wl_index), "wl", perm=swap)
    optic_low = jnp.where(wl_index == 0, optic_mine, optic_theirs)
    optic_high = jnp.where(wl_index == 0, optic_theirs, optic_mine)
    optic_got = jnp.concatenate([optic_low, optic_high], 0)
    spec = forward_cols(got)

    width = spec.shape[-1]
    lane_ids = ids(width)
    itself = jnp.logical_and(first_row, wl_index == 0)
    itself = jnp.logical_and(itself, lane_ids % (width // 2) == 0)
    combined = combine(spec, optic_got, weights, itself)

    back = inverse_cols(combined)
    back = back.reshape((2, row_count, rows_here, width))
    returned = lax.all_to_all(back, "row", split_axis=1, concat_axis=1, tiled=True)
    other = lax.ppermute(returned, "wl", perm=swap)
    returned = join_lanes(returned, other, wl_index)
    returned = groups_to_canon(returned, mcount, 1)
    k_half = across // 2
    return inverse_rows(returned, length, norm_factor, k_half, wl_index * k_half)


def local(scenes, optics, weights):
    row_count = lax.axis_size("row")
    length = scenes.shape[2]
    span = length // 2 // row_count
    if lax.axis_size("wl") == 2 and span % 2 == 0:
        return local_split(scenes, optics, weights)
    norm_factor = 1.0 / (float(length) * float(length))
    wl_index = lax.axis_index("wl")
    local_waves = optics.shape[0]
    weight_rows = lax.dynamic_slice_in_dim(weights, wl_index * local_waves, local_waves, 0)
    first_row = lax.axis_index("row") == 0
    canon = forward_rows(scenes)
    mcount = canon.shape[0]
    sent = canon_to_groups(canon, row_count)
    got = lax.all_to_all(sent, "row", split_axis=0, concat_axis=2, tiled=True)[0]
    spec = forward_cols(got)
    optic_grouped = canon_to_groups(pair_optics(optics), row_count)
    optic_got = lax.all_to_all(optic_grouped, "row", split_axis=0, concat_axis=3, tiled=True)[0]
    width = spec.shape[-1]
    itself = jnp.logical_and(first_row, ids(width) % (width // 2) == 0)
    combined = combine(spec, optic_got, weight_rows, itself)
    back = inverse_cols(combined)
    rows_here = scenes.shape[1]
    back = back.reshape((2, row_count, rows_here, width))
    returned = lax.all_to_all(back, "row", split_axis=1, concat_axis=1, tiled=True)
    returned = groups_to_canon(returned, mcount, 1)
    result_image = inverse_rows(returned, length, norm_factor)
    return lax.psum_scatter(result_image, "wl", scatter_dimension=2, tiled=True)


def solution(mesh):
    in_specs = (P(None, "row", None), P("wl", None, "row", None), P())
    out_specs = P(None, "row", "wl")
    return jax.shard_map(local, mesh=mesh, in_specs=in_specs, out_specs=out_specs, check_vma=False)
```

```python
import math

import jax
import jax.numpy as jnp
from jax import lax
from jax.sharding import PartitionSpec as P

PRECISE = lax.Precision.HIGHEST
NARROW = 32


def phase(left_ids, right_ids, modulus, orient):
    turns = (left_ids * right_ids % modulus).astype(jnp.float32)
    angles = turns * (orient * 2.0 * math.pi / modulus)
    return (jnp.cos(angles), jnp.sin(angles))


def ids(count):
    return jnp.arange(count, dtype=jnp.int32)


def cblock(cos_part, sin_part):
    return jnp.stack([jnp.stack([cos_part, -sin_part]), jnp.stack([sin_part, cos_part])])


def small_tables(out_count, in_count, modulus, orients):
    tables = []
    for orient in orients:
        cos_part, sin_part = phase(ids(out_count)[:, None], ids(in_count)[None, :], modulus, orient)
        tables.append(cblock(cos_part, sin_part))
    return jnp.stack(tables)


def twist(values, axis_e, cos_part, sin_part):
    real = jnp.take(values, 0, axis=axis_e)
    imag = jnp.take(values, 1, axis=axis_e)
    return jnp.stack([real * cos_part - imag * sin_part, real * sin_part + imag * cos_part], axis_e)


def canon_to_groups(canon, group_count):
    mcount, span_c = canon.shape[0], canon.shape[-1] // 2
    mid = canon.shape[1:-1]
    if group_count == mcount:
        return canon
    span = mcount * span_c // group_count
    flat = jnp.moveaxis(canon.reshape((mcount,) + mid + (2, span_c)), 0, -2)
    flat = flat.reshape(mid + (2, group_count, span))
    return jnp.moveaxis(flat, -2, 0).reshape((group_count,) + mid + (2 * span,))


def groups_to_canon(grouped, mcount, axis_g):
    group_count = grouped.shape[axis_g]
    if group_count == mcount:
        return grouped
    moved = jnp.moveaxis(grouped, axis_g, 0)
    mid = moved.shape[1:-1]
    span = moved.shape[-1] // 2
    span_c = group_count * span // mcount
    flat = jnp.moveaxis(moved.reshape((group_count,) + mid + (2, span)), 0, -2)
    flat = flat.reshape(mid + (2, mcount, span_c))
    canon = jnp.moveaxis(flat, -2, 0).reshape((mcount,) + mid + (2 * span_c,))
    return jnp.moveaxis(canon, 0, axis_g)


def forward_rows(scenes):
    rows_here, length = scenes.shape[1], scenes.shape[2]
    across = length // NARROW
    half_k = across // 2
    grid = scenes.reshape((2, rows_here, NARROW, across))
    first_tab = jnp.transpose(small_tables(NARROW, NARROW, NARROW, (-1.0, 1.0)), (0, 3, 1, 2, 4))
    first = jnp.einsum("oaedb,drbn->oaern", first_tab, grid, precision=PRECISE)
    tw_cos, tw_sin = [], []
    for orient in (-1.0, 1.0):
        cos_part, sin_part = phase(ids(NARROW)[:, None], ids(across)[None, :], length, orient)
        tw_cos.append(cos_part)
        tw_sin.append(sin_part)
    tw_cos = jnp.stack(tw_cos)[:, :, None, :]
    tw_sin = jnp.stack(tw_sin)[:, :, None, :]
    turned = twist(first, 2, tw_cos, tw_sin)
    second_tab = jnp.transpose(small_tables(half_k, across, across, (-1.0, 1.0)), (0, 2, 4, 1, 3))
    second = jnp.einsum("oaern,oenfk->oarfk", turned, second_tab, precision=PRECISE)
    signs = 1.0 - 2.0 * (ids(across) % 2).astype(jnp.float32)
    nyquist = jnp.einsum("ern,n->er", first[0, 0], signs, precision=PRECISE)
    per_block = across // NARROW
    mcount = half_k // per_block
    blocks = second.reshape((2, NARROW, rows_here, 2, mcount, per_block))
    canon = jnp.transpose(blocks, (4, 3, 2, 0, 5, 1)).reshape((mcount, 2, rows_here, 2 * across))
    canon = canon.at[0, :, :, across].set(nyquist)
    return canon


def forward_cols(columns):
    length, width = columns.shape[1], columns.shape[2]
    across = length // NARROW
    grid = columns.reshape((2, NARROW, across, width))
    first_tab = jnp.transpose(small_tables(NARROW, NARROW, NARROW, (-1.0, 1.0)), (0, 3, 1, 2, 4))
    first = jnp.einsum("oafeb,ebnj->oafnj", first_tab, grid, precision=PRECISE)
    tw_cos, tw_sin = [], []
    for orient in (-1.0, 1.0):
        cos_part, sin_part = phase(ids(NARROW)[:, None], ids(across)[None, :], length, orient)
        tw_cos.append(cos_part)
        tw_sin.append(sin_part)
    tw_cos = jnp.stack(tw_cos)[:, :, :, None]
    tw_sin = jnp.stack(tw_sin)[:, :, :, None]
    turned = twist(first, 2, tw_cos, tw_sin)
    second_tab = small_tables(across, across, across, (-1.0, 1.0))
    second = jnp.einsum("ofekn,oaenj->ofkaj", second_tab, turned, precision=PRECISE)
    return second.reshape((2, 2, length, width))


def inverse_cols(combined):
    length, width = combined.shape[1], combined.shape[2]
    across = length // NARROW
    grid = combined.reshape((2, NARROW, across, width))
    first_tab = jnp.transpose(small_tables(NARROW, NARROW, NARROW, (1.0,))[0], (2, 0, 1, 3))
    first = jnp.einsum("afeb,ebnj->afnj", first_tab, grid, precision=PRECISE)
    cos_part, sin_part = phase(ids(NARROW)[:, None], ids(across)[None, :], length, 1.0)
    turned = twist(first, 1, cos_part[:, :, None], sin_part[:, :, None])
    second_tab = jnp.transpose(small_tables(across, across, across, (1.0,))[0], (0, 2, 1, 3))
    second = jnp.einsum("fken,aenj->fkaj", second_tab, turned, precision=PRECISE)
    return second.reshape((2, length, width))


def inverse_rows(canon, length, scale):
    mcount, rows_here, width = canon.shape[1], canon.shape[2], canon.shape[3]
    across = width // 2
    first_tab = jnp.transpose(small_tables(NARROW, mcount, NARROW, (1.0, -1.0)), (0, 3, 1, 2, 4))
    first = jnp.einsum("oafem,emRj->oafRj", first_tab, canon, precision=PRECISE)
    lower = first[0, :, :, :, :across]
    upper = first[1, :, :, :, across:]
    flip_gain = -2.0 * (ids(NARROW) % 2).astype(jnp.float32)
    fix = flip_gain[:, None, None] * canon[:, 0, :, across][None]
    lane0 = (ids(across) == 0)[None, None, None, :]
    upper = jnp.where(lane0, upper + fix[..., None], upper)
    cos_up, sin_up = phase(ids(NARROW)[:, None], ids(across)[None, :], length, 1.0)
    cos_dn, sin_dn = phase(ids(NARROW)[:, None], ids(across)[None, :], length, -1.0)
    lower = twist(lower, 1, cos_up[:, None, :], sin_up[:, None, :])
    upper = twist(upper, 1, cos_dn[:, None, :], sin_dn[:, None, :])
    tabs = small_tables(across, across, across, (1.0, -1.0)) * scale
    tabs = jnp.transpose(tabs, (0, 2, 4, 1, 3))
    out = jnp.einsum("aeRu,eufk->aRfk", lower, tabs[0], precision=PRECISE)
    out = out + jnp.einsum("aeRu,eufk->aRfk", upper, tabs[1], precision=PRECISE)
    return jnp.transpose(out, (2, 1, 3, 0)).reshape((2, rows_here, length))


def pair_optics(optics):
    length = optics.shape[-1]
    across = length // NARROW
    half = length // 2
    mcount = half // across
    block = [lax.slice_in_dim(optics, across * i, across * (i + 1), axis=3) for i in range(NARROW)]
    windows = []
    for m in range(mcount):
        second = block[(half // across) if m == 0 else (NARROW - m)]
        windows.append(jnp.concatenate([block[NARROW - 1 - m], second], -1))
    windows = jnp.stack(windows)
    src = ids(2 * across)[:, None]
    dst = ids(across)[None, :]
    picker = jnp.logical_or(
        jnp.logical_and(src == across - dst, dst > 0), jnp.logical_and(src == across, dst == 0)
    ).astype(optics.dtype)
    mirrored = jnp.einsum("mwcpv,vu->mwcpu", windows, picker, preferred_element_type=jnp.float32)
    lower = jnp.stack(block[:mcount])
    return jnp.concatenate([lower, mirrored.astype(optics.dtype)], -1)


def local(scenes, optics, weights):
    row_count = lax.axis_size("row")
    length = scenes.shape[2]
    across = length // NARROW
    norm_factor = 1.0 / (float(length) * float(length))
    wl_index = lax.axis_index("wl")
    local_waves = optics.shape[0]
    weight_rows = lax.dynamic_slice_in_dim(weights, wl_index * local_waves, local_waves, 0)
    first_row = lax.axis_index("row") == 0

    wl_count = lax.axis_size("wl")
    rows_here = scenes.shape[1]
    own_rows = rows_here // wl_count
    if wl_count == 2 and own_rows * wl_count == rows_here:
        mine = lax.dynamic_slice_in_dim(scenes, wl_index * own_rows, own_rows, 1)
        canon = forward_rows(mine)
        mcount = canon.shape[0]
        sent = canon_to_groups(canon, row_count)
        got = lax.all_to_all(sent, "row", split_axis=0, concat_axis=2, tiled=True)[0]
        other = lax.ppermute(got, "wl", perm=[(0, 1), (1, 0)])
        got = got.reshape((2, row_count, own_rows, got.shape[-1]))
        other = other.reshape(got.shape)
        first_half = jnp.where(wl_index == 0, got, other)
        second_half = jnp.where(wl_index == 0, other, got)
        got = jnp.stack([first_half, second_half], 2).reshape((2, length, got.shape[-1]))
    else:
        canon = forward_rows(scenes)
        mcount = canon.shape[0]
        sent = canon_to_groups(canon, row_count)
        got = lax.all_to_all(sent, "row", split_axis=0, concat_axis=2, tiled=True)[0]
    spec = forward_cols(got)

    optic_canon = pair_optics(optics)
    optic_sent = canon_to_groups(optic_canon, row_count)
    optic_got = lax.all_to_all(optic_sent, "row", split_axis=0, concat_axis=3, tiled=True)[0]

    width = spec.shape[-1]
    span = width // 2
    lane_ids = ids(width)
    itself = jnp.logical_and(first_row, lane_ids % span == 0)
    direct = spec[0]
    flipped = spec[1]
    swapped = jnp.concatenate([flipped[..., span:], flipped[..., :span]], -1)
    partner = jnp.where(itself, flipped, swapped)
    mirror_real = partner[0]
    mirror_imag = -partner[1]
    even_real = 0.5 * (direct[0] + mirror_real)
    even_imag = 0.5 * (direct[1] + mirror_imag)
    odd_real = 0.5 * (direct[0] - mirror_real)
    odd_imag = 0.5 * (direct[1] - mirror_imag)
    combined_real = jnp.zeros_like(even_real)
    combined_imag = jnp.zeros_like(even_imag)
    for colour in range(local_waves):
        mixed_real = weight_rows[colour, 0] * even_real + weight_rows[colour, 1] * odd_real
        mixed_imag = weight_rows[colour, 0] * even_imag + weight_rows[colour, 1] * odd_imag
        resp_real = optic_got[colour, 0].astype(jnp.float32)
        resp_imag = optic_got[colour, 1].astype(jnp.float32)
        combined_real = combined_real + resp_real * mixed_real - resp_imag * mixed_imag
        combined_imag = combined_imag + resp_real * mixed_imag + resp_imag * mixed_real

    back = inverse_cols(jnp.stack([combined_real, combined_imag]))
    if wl_count != 2 or own_rows * wl_count != rows_here:
        back = back.reshape((2, row_count, rows_here, width))
        returned = lax.all_to_all(back, "row", split_axis=1, concat_axis=1, tiled=True)
        returned = groups_to_canon(returned, mcount, 1)
        result_image = inverse_rows(returned, length, norm_factor)
        return lax.psum_scatter(result_image, "wl", scatter_dimension=2, tiled=True)
    back = back.reshape((2, row_count, 2, own_rows, width))
    kept = lax.dynamic_index_in_dim(back, wl_index, 2, keepdims=False)
    given = lax.dynamic_index_in_dim(back, 1 - wl_index, 2, keepdims=False)
    half = length // 2
    pieces = 2 if own_rows % 16 == 0 else 1
    piece_rows = own_rows // pieces
    mines, takens = [], []
    for piece in range(pieces):
        rows = slice(piece * piece_rows, (piece + 1) * piece_rows)
        summed = kept[:, :, rows] + lax.ppermute(given[:, :, rows], "wl", perm=[(0, 1), (1, 0)])
        returned = lax.all_to_all(summed, "row", split_axis=1, concat_axis=1, tiled=True)
        returned = groups_to_canon(returned, mcount, 1)
        result_image = inverse_rows(returned, length, norm_factor)
        result_image = result_image.reshape((2, piece_rows, 2, half))
        mines.append(lax.dynamic_index_in_dim(result_image, wl_index, 2, keepdims=False))
        theirs = lax.dynamic_index_in_dim(result_image, 1 - wl_index, 2, keepdims=False)
        takens.append(lax.ppermute(theirs, "wl", perm=[(0, 1), (1, 0)]))
    mine = jnp.concatenate(mines, 1)
    taken = jnp.concatenate(takens, 1)
    upper = jnp.where(wl_index == 0, mine, taken)
    lower = jnp.where(wl_index == 0, taken, mine)
    return jnp.concatenate([upper, lower], 1)


def solution(mesh):
    in_specs = (P(None, "row", None), P("wl", None, "row", None), P())
    out_specs = P(None, "row", "wl")
    return jax.shard_map(local, mesh=mesh, in_specs=in_specs, out_specs=out_specs, check_vma=False)
```

```python
import math

import jax
import jax.numpy as jnp
from jax import lax
from jax.sharding import PartitionSpec as P

PRECISE = lax.Precision.HIGHEST
NARROW = 32


def phase(left_ids, right_ids, modulus, orient):
    turns = (left_ids * right_ids % modulus).astype(jnp.float32)
    angles = turns * (orient * 2.0 * math.pi / modulus)
    return (jnp.cos(angles), jnp.sin(angles))


def ids(count):
    return jnp.arange(count, dtype=jnp.int32)


def cblock(cos_part, sin_part):
    return jnp.stack([jnp.stack([cos_part, -sin_part]), jnp.stack([sin_part, cos_part])])


def small_tables(out_count, in_count, modulus, orients):
    tables = []
    for orient in orients:
        cos_part, sin_part = phase(ids(out_count)[:, None], ids(in_count)[None, :], modulus, orient)
        tables.append(cblock(cos_part, sin_part))
    return jnp.stack(tables)


def twist(values, axis_e, cos_part, sin_part):
    real = jnp.take(values, 0, axis=axis_e)
    imag = jnp.take(values, 1, axis=axis_e)
    return jnp.stack([real * cos_part - imag * sin_part, real * sin_part + imag * cos_part], axis_e)


def canon_to_groups(canon, group_count):
    mcount, span_c = canon.shape[0], canon.shape[-1] // 2
    mid = canon.shape[1:-1]
    if group_count == mcount:
        return canon
    span = mcount * span_c // group_count
    flat = jnp.moveaxis(canon.reshape((mcount,) + mid + (2, span_c)), 0, -2)
    flat = flat.reshape(mid + (2, group_count, span))
    return jnp.moveaxis(flat, -2, 0).reshape((group_count,) + mid + (2 * span,))


def groups_to_canon(grouped, mcount, axis_g):
    group_count = grouped.shape[axis_g]
    if group_count == mcount:
        return grouped
    moved = jnp.moveaxis(grouped, axis_g, 0)
    mid = moved.shape[1:-1]
    span = moved.shape[-1] // 2
    span_c = group_count * span // mcount
    flat = jnp.moveaxis(moved.reshape((group_count,) + mid + (2, span)), 0, -2)
    flat = flat.reshape(mid + (2, mcount, span_c))
    canon = jnp.moveaxis(flat, -2, 0).reshape((mcount,) + mid + (2 * span_c,))
    return jnp.moveaxis(canon, 0, axis_g)


def forward_rows(scenes):
    rows_here, length = scenes.shape[1], scenes.shape[2]
    across = length // NARROW
    half_k = across // 2
    grid = scenes.reshape((2, rows_here, NARROW, across))
    first_tab = jnp.transpose(small_tables(NARROW, NARROW, NARROW, (-1.0, 1.0)), (0, 3, 1, 2, 4))
    first = jnp.einsum("oaedb,drbn->oaern", first_tab, grid, precision=PRECISE)
    tw_cos, tw_sin = [], []
    for orient in (-1.0, 1.0):
        cos_part, sin_part = phase(ids(NARROW)[:, None], ids(across)[None, :], length, orient)
        tw_cos.append(cos_part)
        tw_sin.append(sin_part)
    tw_cos = jnp.stack(tw_cos)[:, :, None, :]
    tw_sin = jnp.stack(tw_sin)[:, :, None, :]
    turned = twist(first, 2, tw_cos, tw_sin)
    second_tab = jnp.transpose(small_tables(half_k, across, across, (-1.0, 1.0)), (0, 2, 4, 1, 3))
    second = jnp.einsum("oaern,oenfk->oarfk", turned, second_tab, precision=PRECISE)
    signs = 1.0 - 2.0 * (ids(across) % 2).astype(jnp.float32)
    nyquist = jnp.einsum("ern,n->er", first[0, 0], signs, precision=PRECISE)
    per_block = across // NARROW
    mcount = half_k // per_block
    blocks = second.reshape((2, NARROW, rows_here, 2, mcount, per_block))
    canon = jnp.transpose(blocks, (4, 3, 2, 0, 5, 1)).reshape((mcount, 2, rows_here, 2 * across))
    canon = canon.at[0, :, :, across].set(nyquist)
    return canon


def forward_cols(columns):
    length, width = columns.shape[1], columns.shape[2]
    across = length // NARROW
    grid = columns.reshape((2, NARROW, across, width))
    first_tab = jnp.transpose(small_tables(NARROW, NARROW, NARROW, (-1.0, 1.0)), (0, 3, 1, 2, 4))
    first = jnp.einsum("oafeb,ebnj->oafnj", first_tab, grid, precision=PRECISE)
    tw_cos, tw_sin = [], []
    for orient in (-1.0, 1.0):
        cos_part, sin_part = phase(ids(NARROW)[:, None], ids(across)[None, :], length, orient)
        tw_cos.append(cos_part)
        tw_sin.append(sin_part)
    tw_cos = jnp.stack(tw_cos)[:, :, :, None]
    tw_sin = jnp.stack(tw_sin)[:, :, :, None]
    turned = twist(first, 2, tw_cos, tw_sin)
    second_tab = small_tables(across, across, across, (-1.0, 1.0))
    second = jnp.einsum("ofekn,oaenj->ofkaj", second_tab, turned, precision=PRECISE)
    return second.reshape((2, 2, length, width))


def inverse_cols(combined):
    length, width = combined.shape[1], combined.shape[2]
    across = length // NARROW
    grid = combined.reshape((2, NARROW, across, width))
    first_tab = jnp.transpose(small_tables(NARROW, NARROW, NARROW, (1.0,))[0], (2, 0, 1, 3))
    first = jnp.einsum("afeb,ebnj->afnj", first_tab, grid, precision=PRECISE)
    cos_part, sin_part = phase(ids(NARROW)[:, None], ids(across)[None, :], length, 1.0)
    turned = twist(first, 1, cos_part[:, :, None], sin_part[:, :, None])
    second_tab = jnp.transpose(small_tables(across, across, across, (1.0,))[0], (0, 2, 1, 3))
    second = jnp.einsum("fken,aenj->fkaj", second_tab, turned, precision=PRECISE)
    return second.reshape((2, length, width))


def inverse_rows(canon, length, scale, k_count=None, k_start=0):
    mcount, rows_here, width = canon.shape[1], canon.shape[2], canon.shape[3]
    across = width // 2
    k_count = across if k_count is None else k_count
    first_tab = jnp.transpose(small_tables(NARROW, mcount, NARROW, (1.0, -1.0)), (0, 3, 1, 2, 4))
    first = jnp.einsum("oafem,emRj->oafRj", first_tab, canon, precision=PRECISE)
    lower = first[0, :, :, :, :across]
    upper = first[1, :, :, :, across:]
    flip_gain = -2.0 * (ids(NARROW) % 2).astype(jnp.float32)
    fix = flip_gain[:, None, None] * canon[:, 0, :, across][None]
    lane0 = (ids(across) == 0)[None, None, None, :]
    upper = jnp.where(lane0, upper + fix[..., None], upper)
    cos_up, sin_up = phase(ids(NARROW)[:, None], ids(across)[None, :], length, 1.0)
    cos_dn, sin_dn = phase(ids(NARROW)[:, None], ids(across)[None, :], length, -1.0)
    lower = twist(lower, 1, cos_up[:, None, :], sin_up[:, None, :])
    upper = twist(upper, 1, cos_dn[:, None, :], sin_dn[:, None, :])
    tabs = []
    for orient in (1.0, -1.0):
        k_ids = ids(k_count)[:, None] + k_start
        cos_part, sin_part = phase(k_ids, ids(across)[None, :], across, orient)
        tabs.append(cblock(cos_part, sin_part))
    tabs = jnp.transpose(jnp.stack(tabs) * scale, (0, 2, 4, 1, 3))
    out = jnp.einsum("aeRu,eufk->aRfk", lower, tabs[0], precision=PRECISE)
    out = out + jnp.einsum("aeRu,eufk->aRfk", upper, tabs[1], precision=PRECISE)
    return jnp.transpose(out, (2, 1, 3, 0)).reshape((2, rows_here, k_count * NARROW))


def pair_optics(optics):
    length = optics.shape[-1]
    across = length // NARROW
    half = length // 2
    mcount = half // across
    block = [lax.slice_in_dim(optics, across * i, across * (i + 1), axis=3) for i in range(NARROW)]
    windows = []
    for m in range(mcount):
        second = block[(half // across) if m == 0 else (NARROW - m)]
        windows.append(jnp.concatenate([block[NARROW - 1 - m], second], -1))
    windows = jnp.stack(windows)
    src = ids(2 * across)[:, None]
    dst = ids(across)[None, :]
    picker = jnp.logical_or(
        jnp.logical_and(src == across - dst, dst > 0), jnp.logical_and(src == across, dst == 0)
    ).astype(optics.dtype)
    mirrored = jnp.einsum("mwcpv,vu->mwcpu", windows, picker, preferred_element_type=jnp.float32)
    lower = jnp.stack(block[:mcount])
    return jnp.concatenate([lower, mirrored.astype(optics.dtype)], -1)


def local(scenes, optics, weights):
    row_count = lax.axis_size("row")
    length = scenes.shape[2]
    across = length // NARROW
    norm_factor = 1.0 / (float(length) * float(length))
    wl_index = lax.axis_index("wl")
    local_waves = optics.shape[0]
    weight_rows = lax.dynamic_slice_in_dim(weights, wl_index * local_waves, local_waves, 0)
    first_row = lax.axis_index("row") == 0

    wl_count = lax.axis_size("wl")
    rows_here = scenes.shape[1]
    own_rows = rows_here // wl_count
    if wl_count == 2 and own_rows * wl_count == rows_here:
        mine = lax.dynamic_slice_in_dim(scenes, wl_index * own_rows, own_rows, 1)
        canon = forward_rows(mine)
        mcount = canon.shape[0]
        sent = canon_to_groups(canon, row_count)
        got = lax.all_to_all(sent, "row", split_axis=0, concat_axis=2, tiled=True)[0]
        other = lax.ppermute(got, "wl", perm=[(0, 1), (1, 0)])
        got = got.reshape((2, row_count, own_rows, got.shape[-1]))
        other = other.reshape(got.shape)
        first_half = jnp.where(wl_index == 0, got, other)
        second_half = jnp.where(wl_index == 0, other, got)
        got = jnp.stack([first_half, second_half], 2).reshape((2, length, got.shape[-1]))
    else:
        canon = forward_rows(scenes)
        mcount = canon.shape[0]
        sent = canon_to_groups(canon, row_count)
        got = lax.all_to_all(sent, "row", split_axis=0, concat_axis=2, tiled=True)[0]
    spec = forward_cols(got)

    optic_canon = pair_optics(optics)
    optic_sent = canon_to_groups(optic_canon, row_count)
    optic_got = lax.all_to_all(optic_sent, "row", split_axis=0, concat_axis=3, tiled=True)[0]

    width = spec.shape[-1]
    span = width // 2
    lane_ids = ids(width)
    itself = jnp.logical_and(first_row, lane_ids % span == 0)
    direct = spec[0]
    flipped = spec[1]
    swapped = jnp.concatenate([flipped[..., span:], flipped[..., :span]], -1)
    partner = jnp.where(itself, flipped, swapped)
    mirror_real = partner[0]
    mirror_imag = -partner[1]
    even_real = 0.5 * (direct[0] + mirror_real)
    even_imag = 0.5 * (direct[1] + mirror_imag)
    odd_real = 0.5 * (direct[0] - mirror_real)
    odd_imag = 0.5 * (direct[1] - mirror_imag)
    combined_real = jnp.zeros_like(even_real)
    combined_imag = jnp.zeros_like(even_imag)
    for colour in range(local_waves):
        mixed_real = weight_rows[colour, 0] * even_real + weight_rows[colour, 1] * odd_real
        mixed_imag = weight_rows[colour, 0] * even_imag + weight_rows[colour, 1] * odd_imag
        resp_real = optic_got[colour, 0].astype(jnp.float32)
        resp_imag = optic_got[colour, 1].astype(jnp.float32)
        combined_real = combined_real + resp_real * mixed_real - resp_imag * mixed_imag
        combined_imag = combined_imag + resp_real * mixed_imag + resp_imag * mixed_real

    back = inverse_cols(jnp.stack([combined_real, combined_imag]))
    if wl_count != 2 or own_rows * wl_count != rows_here:
        back = back.reshape((2, row_count, rows_here, width))
        returned = lax.all_to_all(back, "row", split_axis=1, concat_axis=1, tiled=True)
        returned = groups_to_canon(returned, mcount, 1)
        result_image = inverse_rows(returned, length, norm_factor)
        return lax.psum_scatter(result_image, "wl", scatter_dimension=2, tiled=True)
    back = back.reshape((2, row_count, 2, own_rows, width))
    kept = lax.dynamic_index_in_dim(back, wl_index, 2, keepdims=False)
    given = lax.dynamic_index_in_dim(back, 1 - wl_index, 2, keepdims=False)
    summed = kept + lax.ppermute(given, "wl", perm=[(0, 1), (1, 0)])
    returned = lax.all_to_all(summed, "row", split_axis=1, concat_axis=1, tiled=True)
    returned = groups_to_canon(returned, mcount, 1)
    k_half = across // 2
    theirs = inverse_rows(returned, length, norm_factor, k_half, (1 - wl_index) * k_half)
    taken = lax.ppermute(theirs, "wl", perm=[(0, 1), (1, 0)])
    mine = inverse_rows(returned, length, norm_factor, k_half, wl_index * k_half)
    upper = jnp.where(wl_index == 0, mine, taken)
    lower = jnp.where(wl_index == 0, taken, mine)
    return jnp.concatenate([upper, lower], 1)


def solution(mesh):
    in_specs = (P(None, "row", None), P("wl", None, "row", None), P())
    out_specs = P(None, "row", "wl")
    return jax.shard_map(local, mesh=mesh, in_specs=in_specs, out_specs=out_specs, check_vma=False)
```

```python
import math

import jax
import jax.numpy as jnp
from jax import lax
from jax.sharding import PartitionSpec as P

PRECISE = lax.Precision.HIGHEST
NARROW = 32


def phase(left_ids, right_ids, modulus, orient):
    turns = (left_ids * right_ids % modulus).astype(jnp.float32)
    angles = turns * (orient * 2.0 * math.pi / modulus)
    return (jnp.cos(angles), jnp.sin(angles))


def ids(count):
    return jnp.arange(count, dtype=jnp.int32)


def cblock(cos_part, sin_part):
    return jnp.stack([jnp.stack([cos_part, -sin_part]), jnp.stack([sin_part, cos_part])])


def small_tables(out_count, in_count, modulus, orients):
    tables = []
    for orient in orients:
        cos_part, sin_part = phase(ids(out_count)[:, None], ids(in_count)[None, :], modulus, orient)
        tables.append(cblock(cos_part, sin_part))
    return jnp.stack(tables)


def twist(values, axis_e, cos_part, sin_part):
    real = jnp.take(values, 0, axis=axis_e)
    imag = jnp.take(values, 1, axis=axis_e)
    return jnp.stack([real * cos_part - imag * sin_part, real * sin_part + imag * cos_part], axis_e)


def canon_to_groups(canon, group_count):
    mcount, span_c = canon.shape[0], canon.shape[-1] // 2
    mid = canon.shape[1:-1]
    if group_count == mcount:
        return canon
    span = mcount * span_c // group_count
    flat = jnp.moveaxis(canon.reshape((mcount,) + mid + (2, span_c)), 0, -2)
    flat = flat.reshape(mid + (2, group_count, span))
    return jnp.moveaxis(flat, -2, 0).reshape((group_count,) + mid + (2 * span,))


def groups_to_canon(grouped, mcount, axis_g):
    group_count = grouped.shape[axis_g]
    if group_count == mcount:
        return grouped
    moved = jnp.moveaxis(grouped, axis_g, 0)
    mid = moved.shape[1:-1]
    span = moved.shape[-1] // 2
    span_c = group_count * span // mcount
    flat = jnp.moveaxis(moved.reshape((group_count,) + mid + (2, span)), 0, -2)
    flat = flat.reshape(mid + (2, mcount, span_c))
    canon = jnp.moveaxis(flat, -2, 0).reshape((mcount,) + mid + (2 * span_c,))
    return jnp.moveaxis(canon, 0, axis_g)


def forward_rows(scenes):
    rows_here, length = scenes.shape[1], scenes.shape[2]
    across = length // NARROW
    half_k = across // 2
    grid = scenes.reshape((2, rows_here, NARROW, across))
    first_tab = jnp.transpose(small_tables(NARROW, NARROW, NARROW, (-1.0, 1.0)), (0, 3, 1, 2, 4))
    first = jnp.einsum("oaedb,drbn->oaern", first_tab, grid, precision=PRECISE)
    tw_cos, tw_sin = [], []
    for orient in (-1.0, 1.0):
        cos_part, sin_part = phase(ids(NARROW)[:, None], ids(across)[None, :], length, orient)
        tw_cos.append(cos_part)
        tw_sin.append(sin_part)
    tw_cos = jnp.stack(tw_cos)[:, :, None, :]
    tw_sin = jnp.stack(tw_sin)[:, :, None, :]
    turned = twist(first, 2, tw_cos, tw_sin)
    second_tab = jnp.transpose(small_tables(half_k, across, across, (-1.0, 1.0)), (0, 2, 4, 1, 3))
    second = jnp.einsum("oaern,oenfk->oarfk", turned, second_tab, precision=PRECISE)
    signs = 1.0 - 2.0 * (ids(across) % 2).astype(jnp.float32)
    nyquist = jnp.einsum("ern,n->er", first[0, 0], signs, precision=PRECISE)
    per_block = across // NARROW
    mcount = half_k // per_block
    blocks = second.reshape((2, NARROW, rows_here, 2, mcount, per_block))
    canon = jnp.transpose(blocks, (4, 3, 2, 0, 5, 1)).reshape((mcount, 2, rows_here, 2 * across))
    canon = canon.at[0, :, :, across].set(nyquist)
    return canon


def forward_cols(columns):
    length, width = columns.shape[1], columns.shape[2]
    across = length // NARROW
    grid = columns.reshape((2, NARROW, across, width))
    first_tab = jnp.transpose(small_tables(NARROW, NARROW, NARROW, (-1.0, 1.0)), (0, 3, 1, 2, 4))
    first = jnp.einsum("oafeb,ebnj->oafnj", first_tab, grid, precision=PRECISE)
    tw_cos, tw_sin = [], []
    for orient in (-1.0, 1.0):
        cos_part, sin_part = phase(ids(NARROW)[:, None], ids(across)[None, :], length, orient)
        tw_cos.append(cos_part)
        tw_sin.append(sin_part)
    tw_cos = jnp.stack(tw_cos)[:, :, :, None]
    tw_sin = jnp.stack(tw_sin)[:, :, :, None]
    turned = twist(first, 2, tw_cos, tw_sin)
    second_tab = small_tables(across, across, across, (-1.0, 1.0))
    second = jnp.einsum("ofekn,oaenj->ofkaj", second_tab, turned, precision=PRECISE)
    return second.reshape((2, 2, length, width))


def inverse_cols_half(combined, group_count, half_index):
    length, width = combined.shape[1], combined.shape[2]
    across = length // NARROW
    grid = combined.reshape((2, NARROW, across, width))
    first_tab = jnp.transpose(small_tables(NARROW, NARROW, NARROW, (1.0,))[0], (2, 0, 1, 3))
    first = jnp.einsum("afeb,ebnj->afnj", first_tab, grid, precision=PRECISE)
    cos_part, sin_part = phase(ids(NARROW)[:, None], ids(across)[None, :], length, 1.0)
    turned = twist(first, 1, cos_part[:, :, None], sin_part[:, :, None])
    per_group = across // group_count
    per_half = per_group // 2
    k_ids = ids(group_count)[:, None] * per_group + half_index * per_half + ids(per_half)[None, :]
    cos_k, sin_k = phase(k_ids.reshape((-1, 1)), ids(across)[None, :], across, 1.0)
    second_tab = jnp.transpose(cblock(cos_k, sin_k), (0, 2, 1, 3))
    second = jnp.einsum("fken,aenj->fkaj", second_tab, turned, precision=PRECISE)
    return second.reshape((2, group_count, per_half * NARROW, width))


def inverse_cols(combined):
    length, width = combined.shape[1], combined.shape[2]
    across = length // NARROW
    grid = combined.reshape((2, NARROW, across, width))
    first_tab = jnp.transpose(small_tables(NARROW, NARROW, NARROW, (1.0,))[0], (2, 0, 1, 3))
    first = jnp.einsum("afeb,ebnj->afnj", first_tab, grid, precision=PRECISE)
    cos_part, sin_part = phase(ids(NARROW)[:, None], ids(across)[None, :], length, 1.0)
    turned = twist(first, 1, cos_part[:, :, None], sin_part[:, :, None])
    second_tab = jnp.transpose(small_tables(across, across, across, (1.0,))[0], (0, 2, 1, 3))
    second = jnp.einsum("fken,aenj->fkaj", second_tab, turned, precision=PRECISE)
    return second.reshape((2, length, width))


def inverse_rows(canon, length, scale, k_count=None, k_start=0):
    mcount, rows_here, width = canon.shape[1], canon.shape[2], canon.shape[3]
    across = width // 2
    k_count = across if k_count is None else k_count
    first_tab = jnp.transpose(small_tables(NARROW, mcount, NARROW, (1.0, -1.0)), (0, 3, 1, 2, 4))
    first = jnp.einsum("oafem,emRj->oafRj", first_tab, canon, precision=PRECISE)
    lower = first[0, :, :, :, :across]
    upper = first[1, :, :, :, across:]
    flip_gain = -2.0 * (ids(NARROW) % 2).astype(jnp.float32)
    fix = flip_gain[:, None, None] * canon[:, 0, :, across][None]
    lane0 = (ids(across) == 0)[None, None, None, :]
    upper = jnp.where(lane0, upper + fix[..., None], upper)
    cos_up, sin_up = phase(ids(NARROW)[:, None], ids(across)[None, :], length, 1.0)
    cos_dn, sin_dn = phase(ids(NARROW)[:, None], ids(across)[None, :], length, -1.0)
    lower = twist(lower, 1, cos_up[:, None, :], sin_up[:, None, :])
    upper = twist(upper, 1, cos_dn[:, None, :], sin_dn[:, None, :])
    tabs = []
    for orient in (1.0, -1.0):
        k_ids = ids(k_count)[:, None] + k_start
        cos_part, sin_part = phase(k_ids, ids(across)[None, :], across, orient)
        tabs.append(cblock(cos_part, sin_part))
    tabs = jnp.transpose(jnp.stack(tabs) * scale, (0, 2, 4, 1, 3))
    out = jnp.einsum("aeRu,eufk->aRfk", lower, tabs[0], precision=PRECISE)
    out = out + jnp.einsum("aeRu,eufk->aRfk", upper, tabs[1], precision=PRECISE)
    return jnp.transpose(out, (2, 1, 3, 0)).reshape((2, rows_here, k_count * NARROW))


def pair_optics(optics):
    length = optics.shape[-1]
    across = length // NARROW
    half = length // 2
    mcount = half // across
    block = [lax.slice_in_dim(optics, across * i, across * (i + 1), axis=3) for i in range(NARROW)]
    windows = []
    for m in range(mcount):
        second = block[(half // across) if m == 0 else (NARROW - m)]
        windows.append(jnp.concatenate([block[NARROW - 1 - m], second], -1))
    windows = jnp.stack(windows)
    src = ids(2 * across)[:, None]
    dst = ids(across)[None, :]
    picker = jnp.logical_or(
        jnp.logical_and(src == across - dst, dst > 0), jnp.logical_and(src == across, dst == 0)
    ).astype(optics.dtype)
    mirrored = jnp.einsum("mwcpv,vu->mwcpu", windows, picker, preferred_element_type=jnp.float32)
    lower = jnp.stack(block[:mcount])
    return jnp.concatenate([lower, mirrored.astype(optics.dtype)], -1)


def local(scenes, optics, weights):
    row_count = lax.axis_size("row")
    length = scenes.shape[2]
    across = length // NARROW
    norm_factor = 1.0 / (float(length) * float(length))
    wl_index = lax.axis_index("wl")
    local_waves = optics.shape[0]
    weight_rows = lax.dynamic_slice_in_dim(weights, wl_index * local_waves, local_waves, 0)
    first_row = lax.axis_index("row") == 0

    wl_count = lax.axis_size("wl")
    rows_here = scenes.shape[1]
    own_rows = rows_here // wl_count
    if wl_count == 2 and own_rows * wl_count == rows_here:
        mine = lax.dynamic_slice_in_dim(scenes, wl_index * own_rows, own_rows, 1)
        canon = forward_rows(mine)
        mcount = canon.shape[0]
        sent = canon_to_groups(canon, row_count)
        got = lax.all_to_all(sent, "row", split_axis=0, concat_axis=2, tiled=True)[0]
        other = lax.ppermute(got, "wl", perm=[(0, 1), (1, 0)])
        got = got.reshape((2, row_count, own_rows, got.shape[-1]))
        other = other.reshape(got.shape)
        first_half = jnp.where(wl_index == 0, got, other)
        second_half = jnp.where(wl_index == 0, other, got)
        got = jnp.stack([first_half, second_half], 2).reshape((2, length, got.shape[-1]))
    else:
        canon = forward_rows(scenes)
        mcount = canon.shape[0]
        sent = canon_to_groups(canon, row_count)
        got = lax.all_to_all(sent, "row", split_axis=0, concat_axis=2, tiled=True)[0]
    spec = forward_cols(got)

    optic_canon = pair_optics(optics)
    optic_sent = canon_to_groups(optic_canon, row_count)
    optic_got = lax.all_to_all(optic_sent, "row", split_axis=0, concat_axis=3, tiled=True)[0]

    width = spec.shape[-1]
    span = width // 2
    lane_ids = ids(width)
    itself = jnp.logical_and(first_row, lane_ids % span == 0)
    direct = spec[0]
    flipped = spec[1]
    swapped = jnp.concatenate([flipped[..., span:], flipped[..., :span]], -1)
    partner = jnp.where(itself, flipped, swapped)
    mirror_real = partner[0]
    mirror_imag = -partner[1]
    even_real = 0.5 * (direct[0] + mirror_real)
    even_imag = 0.5 * (direct[1] + mirror_imag)
    odd_real = 0.5 * (direct[0] - mirror_real)
    odd_imag = 0.5 * (direct[1] - mirror_imag)
    combined_real = jnp.zeros_like(even_real)
    combined_imag = jnp.zeros_like(even_imag)
    for colour in range(local_waves):
        mixed_real = weight_rows[colour, 0] * even_real + weight_rows[colour, 1] * odd_real
        mixed_imag = weight_rows[colour, 0] * even_imag + weight_rows[colour, 1] * odd_imag
        resp_real = optic_got[colour, 0].astype(jnp.float32)
        resp_imag = optic_got[colour, 1].astype(jnp.float32)
        combined_real = combined_real + resp_real * mixed_real - resp_imag * mixed_imag
        combined_imag = combined_imag + resp_real * mixed_imag + resp_imag * mixed_real

    stacked = jnp.stack([combined_real, combined_imag])
    back = inverse_cols(stacked)
    if wl_count != 2 or own_rows * wl_count != rows_here:
        back = back.reshape((2, row_count, rows_here, width))
        returned = lax.all_to_all(back, "row", split_axis=1, concat_axis=1, tiled=True)
        returned = groups_to_canon(returned, mcount, 1)
        result_image = inverse_rows(returned, length, norm_factor)
        return lax.psum_scatter(result_image, "wl", scatter_dimension=2, tiled=True)
    per_group = across // row_count
    if per_group % 2 == 0 and per_group * row_count == across:
        given = inverse_cols_half(stacked, row_count, 1 - wl_index)
        incoming = lax.ppermute(given, "wl", perm=[(0, 1), (1, 0)])
        kept = inverse_cols_half(stacked, row_count, wl_index)
    else:
        back = back.reshape((2, row_count, 2, own_rows, width))
        kept = lax.dynamic_index_in_dim(back, wl_index, 2, keepdims=False)
        given = lax.dynamic_index_in_dim(back, 1 - wl_index, 2, keepdims=False)
        incoming = lax.ppermute(given, "wl", perm=[(0, 1), (1, 0)])
    summed = kept + incoming
    returned = lax.all_to_all(summed, "row", split_axis=1, concat_axis=1, tiled=True)
    returned = groups_to_canon(returned, mcount, 1)
    k_half = across // 2
    theirs = inverse_rows(returned, length, norm_factor, k_half, (1 - wl_index) * k_half)
    taken = lax.ppermute(theirs, "wl", perm=[(0, 1), (1, 0)])
    mine = inverse_rows(returned, length, norm_factor, k_half, wl_index * k_half)
    upper = jnp.where(wl_index == 0, mine, taken)
    lower = jnp.where(wl_index == 0, taken, mine)
    return jnp.concatenate([upper, lower], 1)


def solution(mesh):
    in_specs = (P(None, "row", None), P("wl", None, "row", None), P())
    out_specs = P(None, "row", "wl")
    return jax.shard_map(local, mesh=mesh, in_specs=in_specs, out_specs=out_specs, check_vma=False)
```

```python
import math

import jax
import jax.numpy as jnp
from jax import lax
from jax.sharding import PartitionSpec as P

PRECISE = lax.Precision.HIGHEST
NARROW = 32


def phase(left_ids, right_ids, modulus, orient):
    turns = (left_ids * right_ids % modulus).astype(jnp.float32)
    angles = turns * (orient * 2.0 * math.pi / modulus)
    return (jnp.cos(angles), jnp.sin(angles))


def ids(count):
    return jnp.arange(count, dtype=jnp.int32)


def cblock(cos_part, sin_part):
    return jnp.stack([jnp.stack([cos_part, -sin_part]), jnp.stack([sin_part, cos_part])])


def small_tables(out_count, in_count, modulus, orients):
    tables = []
    for orient in orients:
        cos_part, sin_part = phase(ids(out_count)[:, None], ids(in_count)[None, :], modulus, orient)
        tables.append(cblock(cos_part, sin_part))
    return jnp.stack(tables)


def twist(values, axis_e, cos_part, sin_part):
    real = jnp.take(values, 0, axis=axis_e)
    imag = jnp.take(values, 1, axis=axis_e)
    return jnp.stack([real * cos_part - imag * sin_part, real * sin_part + imag * cos_part], axis_e)


def canon_to_groups(canon, group_count):
    mcount, span_c = canon.shape[0], canon.shape[-1] // 2
    mid = canon.shape[1:-1]
    if group_count == mcount:
        return canon
    span = mcount * span_c // group_count
    flat = jnp.moveaxis(canon.reshape((mcount,) + mid + (2, span_c)), 0, -2)
    flat = flat.reshape(mid + (2, group_count, span))
    return jnp.moveaxis(flat, -2, 0).reshape((group_count,) + mid + (2 * span,))


def groups_to_canon(grouped, mcount, axis_g):
    group_count = grouped.shape[axis_g]
    if group_count == mcount:
        return grouped
    moved = jnp.moveaxis(grouped, axis_g, 0)
    mid = moved.shape[1:-1]
    span = moved.shape[-1] // 2
    span_c = group_count * span // mcount
    flat = jnp.moveaxis(moved.reshape((group_count,) + mid + (2, span)), 0, -2)
    flat = flat.reshape(mid + (2, mcount, span_c))
    canon = jnp.moveaxis(flat, -2, 0).reshape((mcount,) + mid + (2 * span_c,))
    return jnp.moveaxis(canon, 0, axis_g)


def forward_rows(scenes):
    rows_here, length = scenes.shape[1], scenes.shape[2]
    across = length // NARROW
    half_k = across // 2
    grid = scenes.reshape((2, rows_here, NARROW, across))
    first_tab = jnp.transpose(small_tables(NARROW, NARROW, NARROW, (-1.0, 1.0)), (0, 3, 1, 2, 4))
    first = jnp.einsum("oaedb,drbn->oaern", first_tab, grid, precision=PRECISE)
    tw_cos, tw_sin = [], []
    for orient in (-1.0, 1.0):
        cos_part, sin_part = phase(ids(NARROW)[:, None], ids(across)[None, :], length, orient)
        tw_cos.append(cos_part)
        tw_sin.append(sin_part)
    tw_cos = jnp.stack(tw_cos)[:, :, None, :]
    tw_sin = jnp.stack(tw_sin)[:, :, None, :]
    turned = twist(first, 2, tw_cos, tw_sin)
    second_tab = jnp.transpose(small_tables(half_k, across, across, (-1.0, 1.0)), (0, 2, 4, 1, 3))
    second = jnp.einsum("oaern,oenfk->oarfk", turned, second_tab, precision=PRECISE)
    signs = 1.0 - 2.0 * (ids(across) % 2).astype(jnp.float32)
    nyquist = jnp.einsum("ern,n->er", first[0, 0], signs, precision=PRECISE)
    per_block = across // NARROW
    mcount = half_k // per_block
    blocks = second.reshape((2, NARROW, rows_here, 2, mcount, per_block))
    canon = jnp.transpose(blocks, (4, 3, 2, 0, 5, 1)).reshape((mcount, 2, rows_here, 2 * across))
    canon = canon.at[0, :, :, across].set(nyquist)
    return canon


def forward_cols(columns):
    length, width = columns.shape[1], columns.shape[2]
    across = length // NARROW
    grid = columns.reshape((2, NARROW, across, width))
    first_tab = jnp.transpose(small_tables(NARROW, NARROW, NARROW, (-1.0, 1.0)), (0, 3, 1, 2, 4))
    first = jnp.einsum("oafeb,ebnj->oafnj", first_tab, grid, precision=PRECISE)
    tw_cos, tw_sin = [], []
    for orient in (-1.0, 1.0):
        cos_part, sin_part = phase(ids(NARROW)[:, None], ids(across)[None, :], length, orient)
        tw_cos.append(cos_part)
        tw_sin.append(sin_part)
    tw_cos = jnp.stack(tw_cos)[:, :, :, None]
    tw_sin = jnp.stack(tw_sin)[:, :, :, None]
    turned = twist(first, 2, tw_cos, tw_sin)
    second_tab = small_tables(across, across, across, (-1.0, 1.0))
    second = jnp.einsum("ofekn,oaenj->ofkaj", second_tab, turned, precision=PRECISE)
    return second.reshape((2, 2, length, width))


def inverse_cols_half(combined, group_count, half_index, part=0, parts=1):
    length, width = combined.shape[1], combined.shape[2]
    across = length // NARROW
    grid = combined.reshape((2, NARROW, across, width))
    first_tab = jnp.transpose(small_tables(NARROW, NARROW, NARROW, (1.0,))[0], (2, 0, 1, 3))
    first = jnp.einsum("afeb,ebnj->afnj", first_tab, grid, precision=PRECISE)
    cos_part, sin_part = phase(ids(NARROW)[:, None], ids(across)[None, :], length, 1.0)
    turned = twist(first, 1, cos_part[:, :, None], sin_part[:, :, None])
    per_group = across // group_count
    per_half = per_group // 2
    per_part = per_half // parts
    k_ids = ids(per_part)[None, :] + part * per_part
    k_ids = ids(group_count)[:, None] * per_group + half_index * per_half + k_ids
    cos_k, sin_k = phase(k_ids.reshape((-1, 1)), ids(across)[None, :], across, 1.0)
    second_tab = jnp.transpose(cblock(cos_k, sin_k), (0, 2, 1, 3))
    second = jnp.einsum("fken,aenj->fkaj", second_tab, turned, precision=PRECISE)
    return second.reshape((2, group_count, per_part * NARROW, width))


def inverse_cols(combined):
    length, width = combined.shape[1], combined.shape[2]
    across = length // NARROW
    grid = combined.reshape((2, NARROW, across, width))
    first_tab = jnp.transpose(small_tables(NARROW, NARROW, NARROW, (1.0,))[0], (2, 0, 1, 3))
    first = jnp.einsum("afeb,ebnj->afnj", first_tab, grid, precision=PRECISE)
    cos_part, sin_part = phase(ids(NARROW)[:, None], ids(across)[None, :], length, 1.0)
    turned = twist(first, 1, cos_part[:, :, None], sin_part[:, :, None])
    second_tab = jnp.transpose(small_tables(across, across, across, (1.0,))[0], (0, 2, 1, 3))
    second = jnp.einsum("fken,aenj->fkaj", second_tab, turned, precision=PRECISE)
    return second.reshape((2, length, width))


def inverse_rows(canon, length, scale, k_count=None, k_start=0):
    mcount, rows_here, width = canon.shape[1], canon.shape[2], canon.shape[3]
    across = width // 2
    k_count = across if k_count is None else k_count
    first_tab = jnp.transpose(small_tables(NARROW, mcount, NARROW, (1.0, -1.0)), (0, 3, 1, 2, 4))
    first = jnp.einsum("oafem,emRj->oafRj", first_tab, canon, precision=PRECISE)
    lower = first[0, :, :, :, :across]
    upper = first[1, :, :, :, across:]
    flip_gain = -2.0 * (ids(NARROW) % 2).astype(jnp.float32)
    fix = flip_gain[:, None, None] * canon[:, 0, :, across][None]
    lane0 = (ids(across) == 0)[None, None, None, :]
    upper = jnp.where(lane0, upper + fix[..., None], upper)
    cos_up, sin_up = phase(ids(NARROW)[:, None], ids(across)[None, :], length, 1.0)
    cos_dn, sin_dn = phase(ids(NARROW)[:, None], ids(across)[None, :], length, -1.0)
    lower = twist(lower, 1, cos_up[:, None, :], sin_up[:, None, :])
    upper = twist(upper, 1, cos_dn[:, None, :], sin_dn[:, None, :])
    tabs = []
    for orient in (1.0, -1.0):
        k_ids = ids(k_count)[:, None] + k_start
        cos_part, sin_part = phase(k_ids, ids(across)[None, :], across, orient)
        tabs.append(cblock(cos_part, sin_part))
    tabs = jnp.transpose(jnp.stack(tabs) * scale, (0, 2, 4, 1, 3))
    out = jnp.einsum("aeRu,eufk->aRfk", lower, tabs[0], precision=PRECISE)
    out = out + jnp.einsum("aeRu,eufk->aRfk", upper, tabs[1], precision=PRECISE)
    return jnp.transpose(out, (2, 1, 3, 0)).reshape((2, rows_here, k_count * NARROW))


def pair_optics(optics):
    length = optics.shape[-1]
    across = length // NARROW
    half = length // 2
    mcount = half // across
    block = [lax.slice_in_dim(optics, across * i, across * (i + 1), axis=3) for i in range(NARROW)]
    windows = []
    for m in range(mcount):
        second = block[(half // across) if m == 0 else (NARROW - m)]
        windows.append(jnp.concatenate([block[NARROW - 1 - m], second], -1))
    windows = jnp.stack(windows)
    src = ids(2 * across)[:, None]
    dst = ids(across)[None, :]
    picker = jnp.logical_or(
        jnp.logical_and(src == across - dst, dst > 0), jnp.logical_and(src == across, dst == 0)
    ).astype(optics.dtype)
    mirrored = jnp.einsum("mwcpv,vu->mwcpu", windows, picker, preferred_element_type=jnp.float32)
    lower = jnp.stack(block[:mcount])
    return jnp.concatenate([lower, mirrored.astype(optics.dtype)], -1)


def local(scenes, optics, weights):
    row_count = lax.axis_size("row")
    length = scenes.shape[2]
    across = length // NARROW
    norm_factor = 1.0 / (float(length) * float(length))
    wl_index = lax.axis_index("wl")
    local_waves = optics.shape[0]
    weight_rows = lax.dynamic_slice_in_dim(weights, wl_index * local_waves, local_waves, 0)
    first_row = lax.axis_index("row") == 0

    wl_count = lax.axis_size("wl")
    rows_here = scenes.shape[1]
    own_rows = rows_here // wl_count
    if wl_count == 2 and own_rows * wl_count == rows_here:
        mine = lax.dynamic_slice_in_dim(scenes, wl_index * own_rows, own_rows, 1)
        canon = forward_rows(mine)
        mcount = canon.shape[0]
        sent = canon_to_groups(canon, row_count)
        got = lax.all_to_all(sent, "row", split_axis=0, concat_axis=2, tiled=True)[0]
        other = lax.ppermute(got, "wl", perm=[(0, 1), (1, 0)])
        got = got.reshape((2, row_count, own_rows, got.shape[-1]))
        other = other.reshape(got.shape)
        first_half = jnp.where(wl_index == 0, got, other)
        second_half = jnp.where(wl_index == 0, other, got)
        got = jnp.stack([first_half, second_half], 2).reshape((2, length, got.shape[-1]))
    else:
        canon = forward_rows(scenes)
        mcount = canon.shape[0]
        sent = canon_to_groups(canon, row_count)
        got = lax.all_to_all(sent, "row", split_axis=0, concat_axis=2, tiled=True)[0]
    spec = forward_cols(got)

    optic_canon = pair_optics(optics)
    optic_sent = canon_to_groups(optic_canon, row_count)
    optic_got = lax.all_to_all(optic_sent, "row", split_axis=0, concat_axis=3, tiled=True)[0]

    width = spec.shape[-1]
    span = width // 2
    lane_ids = ids(width)
    itself = jnp.logical_and(first_row, lane_ids % span == 0)
    direct = spec[0]
    flipped = spec[1]
    swapped = jnp.concatenate([flipped[..., span:], flipped[..., :span]], -1)
    partner = jnp.where(itself, flipped, swapped)
    mirror_real = partner[0]
    mirror_imag = -partner[1]
    even_real = 0.5 * (direct[0] + mirror_real)
    even_imag = 0.5 * (direct[1] + mirror_imag)
    odd_real = 0.5 * (direct[0] - mirror_real)
    odd_imag = 0.5 * (direct[1] - mirror_imag)
    combined_real = jnp.zeros_like(even_real)
    combined_imag = jnp.zeros_like(even_imag)
    for colour in range(local_waves):
        mixed_real = weight_rows[colour, 0] * even_real + weight_rows[colour, 1] * odd_real
        mixed_imag = weight_rows[colour, 0] * even_imag + weight_rows[colour, 1] * odd_imag
        resp_real = optic_got[colour, 0].astype(jnp.float32)
        resp_imag = optic_got[colour, 1].astype(jnp.float32)
        combined_real = combined_real + resp_real * mixed_real - resp_imag * mixed_imag
        combined_imag = combined_imag + resp_real * mixed_imag + resp_imag * mixed_real

    stacked = jnp.stack([combined_real, combined_imag])
    back = inverse_cols(stacked)
    if wl_count != 2 or own_rows * wl_count != rows_here:
        back = back.reshape((2, row_count, rows_here, width))
        returned = lax.all_to_all(back, "row", split_axis=1, concat_axis=1, tiled=True)
        returned = groups_to_canon(returned, mcount, 1)
        result_image = inverse_rows(returned, length, norm_factor)
        return lax.psum_scatter(result_image, "wl", scatter_dimension=2, tiled=True)
    per_group = across // row_count
    if per_group % 2 == 0 and per_group * row_count == across:
        parts = 2 if per_group % 4 == 0 else 1
        incoming = []
        for part in range(parts):
            given = inverse_cols_half(stacked, row_count, 1 - wl_index, part, parts)
            incoming.append(lax.ppermute(given, "wl", perm=[(0, 1), (1, 0)]))
        incoming = jnp.concatenate(incoming, 2)
        kept = inverse_cols_half(stacked, row_count, wl_index)
    else:
        back = back.reshape((2, row_count, 2, own_rows, width))
        kept = lax.dynamic_index_in_dim(back, wl_index, 2, keepdims=False)
        given = lax.dynamic_index_in_dim(back, 1 - wl_index, 2, keepdims=False)
        incoming = lax.ppermute(given, "wl", perm=[(0, 1), (1, 0)])
    summed = kept + incoming
    returned = lax.all_to_all(summed, "row", split_axis=1, concat_axis=1, tiled=True)
    returned = groups_to_canon(returned, mcount, 1)
    k_half = across // 2
    theirs = inverse_rows(returned, length, norm_factor, k_half, (1 - wl_index) * k_half)
    taken = lax.ppermute(theirs, "wl", perm=[(0, 1), (1, 0)])
    mine = inverse_rows(returned, length, norm_factor, k_half, wl_index * k_half)
    upper = jnp.where(wl_index == 0, mine, taken)
    lower = jnp.where(wl_index == 0, taken, mine)
    return jnp.concatenate([upper, lower], 1)


def solution(mesh):
    in_specs = (P(None, "row", None), P("wl", None, "row", None), P())
    out_specs = P(None, "row", "wl")
    return jax.shard_map(local, mesh=mesh, in_specs=in_specs, out_specs=out_specs, check_vma=False)
```

```python
import math

import jax
import jax.numpy as jnp
from jax import lax
from jax.sharding import PartitionSpec as P

PRECISE = lax.Precision.HIGHEST
NARROW = 32


def phase(left_ids, right_ids, modulus, orient):
    turns = (left_ids * right_ids % modulus).astype(jnp.float32)
    angles = turns * (orient * 2.0 * math.pi / modulus)
    return (jnp.cos(angles), jnp.sin(angles))


def ids(count):
    return jnp.arange(count, dtype=jnp.int32)


def cblock(cos_part, sin_part):
    return jnp.stack([jnp.stack([cos_part, -sin_part]), jnp.stack([sin_part, cos_part])])


def small_tables(out_count, in_count, modulus, orients):
    tables = []
    for orient in orients:
        cos_part, sin_part = phase(ids(out_count)[:, None], ids(in_count)[None, :], modulus, orient)
        tables.append(cblock(cos_part, sin_part))
    return jnp.stack(tables)


def twist(values, axis_e, cos_part, sin_part):
    real = jnp.take(values, 0, axis=axis_e)
    imag = jnp.take(values, 1, axis=axis_e)
    return jnp.stack([real * cos_part - imag * sin_part, real * sin_part + imag * cos_part], axis_e)


def canon_to_groups(canon, group_count):
    mcount, span_c = canon.shape[0], canon.shape[-1] // 2
    mid = canon.shape[1:-1]
    if group_count == mcount:
        return canon
    span = mcount * span_c // group_count
    flat = jnp.moveaxis(canon.reshape((mcount,) + mid + (2, span_c)), 0, -2)
    flat = flat.reshape(mid + (2, group_count, span))
    return jnp.moveaxis(flat, -2, 0).reshape((group_count,) + mid + (2 * span,))


def groups_to_canon(grouped, mcount, axis_g):
    group_count = grouped.shape[axis_g]
    if group_count == mcount:
        return grouped
    moved = jnp.moveaxis(grouped, axis_g, 0)
    mid = moved.shape[1:-1]
    span = moved.shape[-1] // 2
    span_c = group_count * span // mcount
    flat = jnp.moveaxis(moved.reshape((group_count,) + mid + (2, span)), 0, -2)
    flat = flat.reshape(mid + (2, mcount, span_c))
    canon = jnp.moveaxis(flat, -2, 0).reshape((mcount,) + mid + (2 * span_c,))
    return jnp.moveaxis(canon, 0, axis_g)


def forward_rows(scenes):
    rows_here, length = scenes.shape[1], scenes.shape[2]
    across = length // NARROW
    half_k = across // 2
    grid = scenes.reshape((2, rows_here, NARROW, across))
    first_tab = jnp.transpose(small_tables(NARROW, NARROW, NARROW, (-1.0, 1.0)), (0, 3, 1, 2, 4))
    first = jnp.einsum("oaedb,drbn->oaern", first_tab, grid, precision=PRECISE)
    tw_cos, tw_sin = [], []
    for orient in (-1.0, 1.0):
        cos_part, sin_part = phase(ids(NARROW)[:, None], ids(across)[None, :], length, orient)
        tw_cos.append(cos_part)
        tw_sin.append(sin_part)
    tw_cos = jnp.stack(tw_cos)[:, :, None, :]
    tw_sin = jnp.stack(tw_sin)[:, :, None, :]
    turned = twist(first, 2, tw_cos, tw_sin)
    second_tab = jnp.transpose(small_tables(half_k, across, across, (-1.0, 1.0)), (0, 2, 4, 1, 3))
    second = jnp.einsum("oaern,oenfk->oarfk", turned, second_tab, precision=PRECISE)
    signs = 1.0 - 2.0 * (ids(across) % 2).astype(jnp.float32)
    nyquist = jnp.einsum("ern,n->er", first[0, 0], signs, precision=PRECISE)
    per_block = across // NARROW
    mcount = half_k // per_block
    blocks = second.reshape((2, NARROW, rows_here, 2, mcount, per_block))
    canon = jnp.transpose(blocks, (4, 3, 2, 0, 5, 1)).reshape((mcount, 2, rows_here, 2 * across))
    canon = canon.at[0, :, :, across].set(nyquist)
    return canon


def forward_cols(columns):
    length, width = columns.shape[1], columns.shape[2]
    across = length // NARROW
    grid = columns.reshape((2, NARROW, across, width))
    first_tab = jnp.transpose(small_tables(NARROW, NARROW, NARROW, (-1.0, 1.0)), (0, 3, 1, 2, 4))
    first = jnp.einsum("oafeb,ebnj->oafnj", first_tab, grid, precision=PRECISE)
    tw_cos, tw_sin = [], []
    for orient in (-1.0, 1.0):
        cos_part, sin_part = phase(ids(NARROW)[:, None], ids(across)[None, :], length, orient)
        tw_cos.append(cos_part)
        tw_sin.append(sin_part)
    tw_cos = jnp.stack(tw_cos)[:, :, :, None]
    tw_sin = jnp.stack(tw_sin)[:, :, :, None]
    turned = twist(first, 2, tw_cos, tw_sin)
    second_tab = small_tables(across, across, across, (-1.0, 1.0))
    second = jnp.einsum("ofekn,oaenj->ofkaj", second_tab, turned, precision=PRECISE)
    return second.reshape((2, 2, length, width))


def inverse_cols_half(combined, group_count, half_index, part=0, parts=1):
    length, width = combined.shape[1], combined.shape[2]
    across = length // NARROW
    grid = combined.reshape((2, NARROW, across, width))
    first_tab = jnp.transpose(small_tables(NARROW, NARROW, NARROW, (1.0,))[0], (2, 0, 1, 3))
    first = jnp.einsum("afeb,ebnj->afnj", first_tab, grid, precision=PRECISE)
    cos_part, sin_part = phase(ids(NARROW)[:, None], ids(across)[None, :], length, 1.0)
    turned = twist(first, 1, cos_part[:, :, None], sin_part[:, :, None])
    per_group = across // group_count
    per_half = per_group // 2
    per_part = per_half // parts
    k_ids = ids(per_part)[None, :] + part * per_part
    k_ids = ids(group_count)[:, None] * per_group + half_index * per_half + k_ids
    cos_k, sin_k = phase(k_ids.reshape((-1, 1)), ids(across)[None, :], across, 1.0)
    second_tab = jnp.transpose(cblock(cos_k, sin_k), (0, 2, 1, 3))
    second = jnp.einsum("fken,aenj->fkaj", second_tab, turned, precision=PRECISE)
    return second.reshape((2, group_count, per_part * NARROW, width))


def inverse_cols(combined):
    length, width = combined.shape[1], combined.shape[2]
    across = length // NARROW
    grid = combined.reshape((2, NARROW, across, width))
    first_tab = jnp.transpose(small_tables(NARROW, NARROW, NARROW, (1.0,))[0], (2, 0, 1, 3))
    first = jnp.einsum("afeb,ebnj->afnj", first_tab, grid, precision=PRECISE)
    cos_part, sin_part = phase(ids(NARROW)[:, None], ids(across)[None, :], length, 1.0)
    turned = twist(first, 1, cos_part[:, :, None], sin_part[:, :, None])
    second_tab = jnp.transpose(small_tables(across, across, across, (1.0,))[0], (0, 2, 1, 3))
    second = jnp.einsum("fken,aenj->fkaj", second_tab, turned, precision=PRECISE)
    return second.reshape((2, length, width))


def inverse_rows(canon, length, scale, k_count=None, k_start=0):
    mcount, rows_here, width = canon.shape[1], canon.shape[2], canon.shape[3]
    across = width // 2
    k_count = across if k_count is None else k_count
    first_tab = jnp.transpose(small_tables(NARROW, mcount, NARROW, (1.0, -1.0)), (0, 3, 1, 2, 4))
    first = jnp.einsum("oafem,emRj->oafRj", first_tab, canon, precision=PRECISE)
    lower = first[0, :, :, :, :across]
    upper = first[1, :, :, :, across:]
    flip_gain = -2.0 * (ids(NARROW) % 2).astype(jnp.float32)
    fix = flip_gain[:, None, None] * canon[:, 0, :, across][None]
    lane0 = (ids(across) == 0)[None, None, None, :]
    upper = jnp.where(lane0, upper + fix[..., None], upper)
    cos_up, sin_up = phase(ids(NARROW)[:, None], ids(across)[None, :], length, 1.0)
    cos_dn, sin_dn = phase(ids(NARROW)[:, None], ids(across)[None, :], length, -1.0)
    lower = twist(lower, 1, cos_up[:, None, :], sin_up[:, None, :])
    upper = twist(upper, 1, cos_dn[:, None, :], sin_dn[:, None, :])
    tabs = []
    for orient in (1.0, -1.0):
        k_ids = ids(k_count)[:, None] + k_start
        cos_part, sin_part = phase(k_ids, ids(across)[None, :], across, orient)
        tabs.append(cblock(cos_part, sin_part))
    tabs = jnp.transpose(jnp.stack(tabs) * scale, (0, 2, 4, 1, 3))
    out = jnp.einsum("aeRu,eufk->aRfk", lower, tabs[0], precision=PRECISE)
    out = out + jnp.einsum("aeRu,eufk->aRfk", upper, tabs[1], precision=PRECISE)
    return jnp.transpose(out, (2, 1, 3, 0)).reshape((2, rows_here, k_count * NARROW))


def pair_optics(optics):
    length = optics.shape[-1]
    across = length // NARROW
    half = length // 2
    mcount = half // across
    block = [lax.slice_in_dim(optics, across * i, across * (i + 1), axis=3) for i in range(NARROW)]
    windows = []
    for m in range(mcount):
        second = block[(half // across) if m == 0 else (NARROW - m)]
        windows.append(jnp.concatenate([block[NARROW - 1 - m], second], -1))
    windows = jnp.stack(windows)
    src = ids(2 * across)[:, None]
    dst = ids(across)[None, :]
    picker = jnp.logical_or(
        jnp.logical_and(src == across - dst, dst > 0), jnp.logical_and(src == across, dst == 0)
    ).astype(optics.dtype)
    mirrored = jnp.einsum("mwcpv,vu->mwcpu", windows, picker, preferred_element_type=jnp.float32)
    lower = jnp.stack(block[:mcount])
    return jnp.concatenate([lower, mirrored.astype(optics.dtype)], -1)


def local(scenes, optics, weights):
    row_count = lax.axis_size("row")
    length = scenes.shape[2]
    across = length // NARROW
    norm_factor = 1.0 / (float(length) * float(length))
    wl_index = lax.axis_index("wl")
    local_waves = optics.shape[0]
    weight_rows = lax.dynamic_slice_in_dim(weights, wl_index * local_waves, local_waves, 0)
    first_row = lax.axis_index("row") == 0

    wl_count = lax.axis_size("wl")
    rows_here = scenes.shape[1]
    own_rows = rows_here // wl_count
    if wl_count == 2 and own_rows * wl_count == rows_here:
        mine = lax.dynamic_slice_in_dim(scenes, wl_index * own_rows, own_rows, 1)
        canon = forward_rows(mine)
        mcount = canon.shape[0]
        sent = canon_to_groups(canon, row_count)
        got = lax.all_to_all(sent, "row", split_axis=0, concat_axis=2, tiled=True)[0]
        other = lax.ppermute(got, "wl", perm=[(0, 1), (1, 0)])
        got = got.reshape((2, row_count, own_rows, got.shape[-1]))
        other = other.reshape(got.shape)
        first_half = jnp.where(wl_index == 0, got, other)
        second_half = jnp.where(wl_index == 0, other, got)
        got = jnp.stack([first_half, second_half], 2).reshape((2, length, got.shape[-1]))
    else:
        canon = forward_rows(scenes)
        mcount = canon.shape[0]
        sent = canon_to_groups(canon, row_count)
        got = lax.all_to_all(sent, "row", split_axis=0, concat_axis=2, tiled=True)[0]
    spec = forward_cols(got)

    optic_canon = pair_optics(optics)
    optic_sent = canon_to_groups(optic_canon, row_count)
    optic_got = lax.all_to_all(optic_sent, "row", split_axis=0, concat_axis=3, tiled=True)[0]

    width = spec.shape[-1]
    span = width // 2
    lane_ids = ids(width)
    itself = jnp.logical_and(first_row, lane_ids % span == 0)
    direct = spec[0]
    flipped = spec[1]
    swapped = jnp.concatenate([flipped[..., span:], flipped[..., :span]], -1)
    partner = jnp.where(itself, flipped, swapped)
    mirror_real = partner[0]
    mirror_imag = -partner[1]
    even_real = 0.5 * (direct[0] + mirror_real)
    even_imag = 0.5 * (direct[1] + mirror_imag)
    odd_real = 0.5 * (direct[0] - mirror_real)
    odd_imag = 0.5 * (direct[1] - mirror_imag)
    combined_real = jnp.zeros_like(even_real)
    combined_imag = jnp.zeros_like(even_imag)
    for colour in range(local_waves):
        mixed_real = weight_rows[colour, 0] * even_real + weight_rows[colour, 1] * odd_real
        mixed_imag = weight_rows[colour, 0] * even_imag + weight_rows[colour, 1] * odd_imag
        resp_real = optic_got[colour, 0].astype(jnp.float32)
        resp_imag = optic_got[colour, 1].astype(jnp.float32)
        combined_real = combined_real + resp_real * mixed_real - resp_imag * mixed_imag
        combined_imag = combined_imag + resp_real * mixed_imag + resp_imag * mixed_real

    stacked = jnp.stack([combined_real, combined_imag])
    back = inverse_cols(stacked)
    if wl_count != 2 or own_rows * wl_count != rows_here:
        back = back.reshape((2, row_count, rows_here, width))
        returned = lax.all_to_all(back, "row", split_axis=1, concat_axis=1, tiled=True)
        returned = groups_to_canon(returned, mcount, 1)
        result_image = inverse_rows(returned, length, norm_factor)
        return lax.psum_scatter(result_image, "wl", scatter_dimension=2, tiled=True)
    per_group = across // row_count
    if per_group % 2 == 0 and per_group * row_count == across:
        parts = 2 if per_group % 4 == 0 else 1
        incoming = []
        for part in range(parts):
            given = inverse_cols_half(stacked, row_count, 1 - wl_index, part, parts)
            incoming.append(lax.ppermute(given, "wl", perm=[(0, 1), (1, 0)]))
        incoming = jnp.concatenate(incoming, 2)
        kept = inverse_cols_half(stacked, row_count, wl_index)
    else:
        back = back.reshape((2, row_count, 2, own_rows, width))
        kept = lax.dynamic_index_in_dim(back, wl_index, 2, keepdims=False)
        given = lax.dynamic_index_in_dim(back, 1 - wl_index, 2, keepdims=False)
        incoming = lax.ppermute(given, "wl", perm=[(0, 1), (1, 0)])
    summed = kept + incoming
    returned = lax.all_to_all(summed, "row", split_axis=1, concat_axis=1, tiled=True)
    returned = groups_to_canon(returned, mcount, 1)
    k_half = across // 2
    k_part = k_half // 2 if k_half % 2 == 0 else k_half
    taken = []
    for k_first in range(0, k_half, k_part):
        theirs = inverse_rows(returned, length, norm_factor, k_part, (1 - wl_index) * k_half + k_first)
        taken.append(lax.ppermute(theirs, "wl", perm=[(0, 1), (1, 0)]))
    taken = jnp.concatenate(taken, 2)
    mine = inverse_rows(returned, length, norm_factor, k_half, wl_index * k_half)
    upper = jnp.where(wl_index == 0, mine, taken)
    lower = jnp.where(wl_index == 0, taken, mine)
    return jnp.concatenate([upper, lower], 1)


def solution(mesh):
    in_specs = (P(None, "row", None), P("wl", None, "row", None), P())
    out_specs = P(None, "row", "wl")
    return jax.shard_map(local, mesh=mesh, in_specs=in_specs, out_specs=out_specs, check_vma=False)
```

```python
import math

import jax
import jax.numpy as jnp
from jax import lax
from jax.sharding import PartitionSpec as P

PRECISE = lax.Precision.HIGHEST
NARROW = 32


def phase(left_ids, right_ids, modulus, orient):
    turns = (left_ids * right_ids % modulus).astype(jnp.float32)
    angles = turns * (orient * 2.0 * math.pi / modulus)
    return (jnp.cos(angles), jnp.sin(angles))


def ids(count):
    return jnp.arange(count, dtype=jnp.int32)


def cblock(cos_part, sin_part):
    return jnp.stack([jnp.stack([cos_part, -sin_part]), jnp.stack([sin_part, cos_part])])


def small_tables(out_count, in_count, modulus, orients):
    tables = []
    for orient in orients:
        cos_part, sin_part = phase(ids(out_count)[:, None], ids(in_count)[None, :], modulus, orient)
        tables.append(cblock(cos_part, sin_part))
    return jnp.stack(tables)


def twist(values, axis_e, cos_part, sin_part):
    real = jnp.take(values, 0, axis=axis_e)
    imag = jnp.take(values, 1, axis=axis_e)
    return jnp.stack([real * cos_part - imag * sin_part, real * sin_part + imag * cos_part], axis_e)


def canon_to_groups(canon, group_count):
    mcount, span_c = canon.shape[0], canon.shape[-1] // 2
    mid = canon.shape[1:-1]
    if group_count == mcount:
        return canon
    span = mcount * span_c // group_count
    flat = jnp.moveaxis(canon.reshape((mcount,) + mid + (2, span_c)), 0, -2)
    flat = flat.reshape(mid + (2, group_count, span))
    return jnp.moveaxis(flat, -2, 0).reshape((group_count,) + mid + (2 * span,))


def groups_to_canon(grouped, mcount, axis_g):
    group_count = grouped.shape[axis_g]
    if group_count == mcount:
        return grouped
    moved = jnp.moveaxis(grouped, axis_g, 0)
    mid = moved.shape[1:-1]
    span = moved.shape[-1] // 2
    span_c = group_count * span // mcount
    flat = jnp.moveaxis(moved.reshape((group_count,) + mid + (2, span)), 0, -2)
    flat = flat.reshape(mid + (2, mcount, span_c))
    canon = jnp.moveaxis(flat, -2, 0).reshape((mcount,) + mid + (2 * span_c,))
    return jnp.moveaxis(canon, 0, axis_g)


def forward_rows(scenes):
    rows_here, length = scenes.shape[1], scenes.shape[2]
    across = length // NARROW
    half_k = across // 2
    grid = scenes.reshape((2, rows_here, NARROW, across))
    first_tab = jnp.transpose(small_tables(NARROW, NARROW, NARROW, (-1.0, 1.0)), (0, 3, 1, 2, 4))
    first = jnp.einsum("oaedb,drbn->oaern", first_tab, grid, precision=PRECISE)
    tw_cos, tw_sin = [], []
    for orient in (-1.0, 1.0):
        cos_part, sin_part = phase(ids(NARROW)[:, None], ids(across)[None, :], length, orient)
        tw_cos.append(cos_part)
        tw_sin.append(sin_part)
    tw_cos = jnp.stack(tw_cos)[:, :, None, :]
    tw_sin = jnp.stack(tw_sin)[:, :, None, :]
    turned = twist(first, 2, tw_cos, tw_sin)
    second_tab = jnp.transpose(small_tables(half_k, across, across, (-1.0, 1.0)), (0, 2, 4, 1, 3))
    second = jnp.einsum("oaern,oenfk->oarfk", turned, second_tab, precision=PRECISE)
    signs = 1.0 - 2.0 * (ids(across) % 2).astype(jnp.float32)
    nyquist = jnp.einsum("ern,n->er", first[0, 0], signs, precision=PRECISE)
    per_block = across // NARROW
    mcount = half_k // per_block
    blocks = second.reshape((2, NARROW, rows_here, 2, mcount, per_block))
    canon = jnp.transpose(blocks, (4, 3, 2, 0, 5, 1)).reshape((mcount, 2, rows_here, 2 * across))
    canon = canon.at[0, :, :, across].set(nyquist)
    return canon


def forward_cols(columns):
    length, width = columns.shape[1], columns.shape[2]
    across = length // NARROW
    grid = columns.reshape((2, NARROW, across, width))
    first_tab = jnp.transpose(small_tables(NARROW, NARROW, NARROW, (-1.0, 1.0)), (0, 3, 1, 2, 4))
    first = jnp.einsum("oafeb,ebnj->oafnj", first_tab, grid, precision=PRECISE)
    tw_cos, tw_sin = [], []
    for orient in (-1.0, 1.0):
        cos_part, sin_part = phase(ids(NARROW)[:, None], ids(across)[None, :], length, orient)
        tw_cos.append(cos_part)
        tw_sin.append(sin_part)
    tw_cos = jnp.stack(tw_cos)[:, :, :, None]
    tw_sin = jnp.stack(tw_sin)[:, :, :, None]
    turned = twist(first, 2, tw_cos, tw_sin)
    second_tab = small_tables(across, across, across, (-1.0, 1.0))
    second = jnp.einsum("ofekn,oaenj->ofkaj", second_tab, turned, precision=PRECISE)
    return second.reshape((2, 2, length, width))


def inverse_cols_half(combined, group_count, half_index, part=0, parts=1):
    length, width = combined.shape[1], combined.shape[2]
    across = length // NARROW
    grid = combined.reshape((2, NARROW, across, width))
    first_tab = jnp.transpose(small_tables(NARROW, NARROW, NARROW, (1.0,))[0], (2, 0, 1, 3))
    first = jnp.einsum("afeb,ebnj->afnj", first_tab, grid, precision=PRECISE)
    cos_part, sin_part = phase(ids(NARROW)[:, None], ids(across)[None, :], length, 1.0)
    turned = twist(first, 1, cos_part[:, :, None], sin_part[:, :, None])
    per_group = across // group_count
    per_half = per_group // 2
    per_part = per_half // parts
    k_ids = ids(per_part)[None, :] + part * per_part
    k_ids = ids(group_count)[:, None] * per_group + half_index * per_half + k_ids
    cos_k, sin_k = phase(k_ids.reshape((-1, 1)), ids(across)[None, :], across, 1.0)
    second_tab = jnp.transpose(cblock(cos_k, sin_k), (0, 2, 1, 3))
    second = jnp.einsum("fken,aenj->fkaj", second_tab, turned, precision=PRECISE)
    return second.reshape((2, group_count, per_part * NARROW, width))


def inverse_cols(combined):
    length, width = combined.shape[1], combined.shape[2]
    across = length // NARROW
    grid = combined.reshape((2, NARROW, across, width))
    first_tab = jnp.transpose(small_tables(NARROW, NARROW, NARROW, (1.0,))[0], (2, 0, 1, 3))
    first = jnp.einsum("afeb,ebnj->afnj", first_tab, grid, precision=PRECISE)
    cos_part, sin_part = phase(ids(NARROW)[:, None], ids(across)[None, :], length, 1.0)
    turned = twist(first, 1, cos_part[:, :, None], sin_part[:, :, None])
    second_tab = jnp.transpose(small_tables(across, across, across, (1.0,))[0], (0, 2, 1, 3))
    second = jnp.einsum("fken,aenj->fkaj", second_tab, turned, precision=PRECISE)
    return second.reshape((2, length, width))


def inverse_rows(canon, length, scale, k_count=None, k_start=0):
    mcount, rows_here, width = canon.shape[1], canon.shape[2], canon.shape[3]
    across = width // 2
    k_count = across if k_count is None else k_count
    first_tab = jnp.transpose(small_tables(NARROW, mcount, NARROW, (1.0, -1.0)), (0, 3, 1, 2, 4))
    first = jnp.einsum("oafem,emRj->oafRj", first_tab, canon, precision=PRECISE)
    lower = first[0, :, :, :, :across]
    upper = first[1, :, :, :, across:]
    flip_gain = -2.0 * (ids(NARROW) % 2).astype(jnp.float32)
    fix = flip_gain[:, None, None] * canon[:, 0, :, across][None]
    lane0 = (ids(across) == 0)[None, None, None, :]
    upper = jnp.where(lane0, upper + fix[..., None], upper)
    cos_up, sin_up = phase(ids(NARROW)[:, None], ids(across)[None, :], length, 1.0)
    cos_dn, sin_dn = phase(ids(NARROW)[:, None], ids(across)[None, :], length, -1.0)
    lower = twist(lower, 1, cos_up[:, None, :], sin_up[:, None, :])
    upper = twist(upper, 1, cos_dn[:, None, :], sin_dn[:, None, :])
    tabs = []
    for orient in (1.0, -1.0):
        k_ids = ids(k_count)[:, None] + k_start
        cos_part, sin_part = phase(k_ids, ids(across)[None, :], across, orient)
        tabs.append(cblock(cos_part, sin_part))
    tabs = jnp.transpose(jnp.stack(tabs) * scale, (0, 2, 4, 1, 3))
    out = jnp.einsum("aeRu,eufk->aRfk", lower, tabs[0], precision=PRECISE)
    out = out + jnp.einsum("aeRu,eufk->aRfk", upper, tabs[1], precision=PRECISE)
    return jnp.transpose(out, (2, 1, 3, 0)).reshape((2, rows_here, k_count * NARROW))


def pair_optics(optics):
    length = optics.shape[-1]
    across = length // NARROW
    half = length // 2
    mcount = half // across
    block = [lax.slice_in_dim(optics, across * i, across * (i + 1), axis=3) for i in range(NARROW)]
    windows = []
    for m in range(mcount):
        second = block[(half // across) if m == 0 else (NARROW - m)]
        windows.append(jnp.concatenate([block[NARROW - 1 - m], second], -1))
    windows = jnp.stack(windows)
    src = ids(2 * across)[:, None]
    dst = ids(across)[None, :]
    picker = jnp.logical_or(
        jnp.logical_and(src == across - dst, dst > 0), jnp.logical_and(src == across, dst == 0)
    ).astype(optics.dtype)
    mirrored = jnp.einsum("mwcpv,vu->mwcpu", windows, picker, preferred_element_type=jnp.float32)
    lower = jnp.stack(block[:mcount])
    return jnp.concatenate([lower, mirrored.astype(optics.dtype)], -1)


def local(scenes, optics, weights):
    row_count = lax.axis_size("row")
    length = scenes.shape[2]
    across = length // NARROW
    norm_factor = 1.0 / (float(length) * float(length))
    wl_index = lax.axis_index("wl")
    local_waves = optics.shape[0]
    weight_rows = lax.dynamic_slice_in_dim(weights, wl_index * local_waves, local_waves, 0)
    first_row = lax.axis_index("row") == 0

    wl_count = lax.axis_size("wl")
    rows_here = scenes.shape[1]
    own_rows = rows_here // wl_count
    if wl_count == 2 and own_rows * wl_count == rows_here:
        mine = lax.dynamic_slice_in_dim(scenes, wl_index * own_rows, own_rows, 1)
        canon = forward_rows(mine)
        mcount = canon.shape[0]
        sent = canon_to_groups(canon, row_count)
        got = lax.all_to_all(sent, "row", split_axis=0, concat_axis=2, tiled=True)[0]
        other = lax.ppermute(got, "wl", perm=[(0, 1), (1, 0)])
        got = got.reshape((2, row_count, own_rows, got.shape[-1]))
        other = other.reshape(got.shape)
        first_half = jnp.where(wl_index == 0, got, other)
        second_half = jnp.where(wl_index == 0, other, got)
        got = jnp.stack([first_half, second_half], 2).reshape((2, length, got.shape[-1]))
    else:
        canon = forward_rows(scenes)
        mcount = canon.shape[0]
        sent = canon_to_groups(canon, row_count)
        got = lax.all_to_all(sent, "row", split_axis=0, concat_axis=2, tiled=True)[0]
    spec = forward_cols(got)

    optic_canon = pair_optics(optics)
    optic_sent = canon_to_groups(optic_canon, row_count)
    optic_got = lax.all_to_all(optic_sent, "row", split_axis=0, concat_axis=3, tiled=True)[0]

    width = spec.shape[-1]
    span = width // 2
    lane_ids = ids(width)
    itself = jnp.logical_and(first_row, lane_ids % span == 0)
    direct = spec[0]
    flipped = spec[1]
    swapped = jnp.concatenate([flipped[..., span:], flipped[..., :span]], -1)
    partner = jnp.where(itself, flipped, swapped)
    mirror_real = partner[0]
    mirror_imag = -partner[1]
    even_real = 0.5 * (direct[0] + mirror_real)
    even_imag = 0.5 * (direct[1] + mirror_imag)
    odd_real = 0.5 * (direct[0] - mirror_real)
    odd_imag = 0.5 * (direct[1] - mirror_imag)
    combined_real = jnp.zeros_like(even_real)
    combined_imag = jnp.zeros_like(even_imag)
    for colour in range(local_waves):
        mixed_real = weight_rows[colour, 0] * even_real + weight_rows[colour, 1] * odd_real
        mixed_imag = weight_rows[colour, 0] * even_imag + weight_rows[colour, 1] * odd_imag
        resp_real = optic_got[colour, 0].astype(jnp.float32)
        resp_imag = optic_got[colour, 1].astype(jnp.float32)
        combined_real = combined_real + resp_real * mixed_real - resp_imag * mixed_imag
        combined_imag = combined_imag + resp_real * mixed_imag + resp_imag * mixed_real

    stacked = jnp.stack([combined_real, combined_imag])
    back = inverse_cols(stacked)
    if wl_count != 2 or own_rows * wl_count != rows_here:
        back = back.reshape((2, row_count, rows_here, width))
        returned = lax.all_to_all(back, "row", split_axis=1, concat_axis=1, tiled=True)
        returned = groups_to_canon(returned, mcount, 1)
        result_image = inverse_rows(returned, length, norm_factor)
        return lax.psum_scatter(result_image, "wl", scatter_dimension=2, tiled=True)
    per_group = across // row_count
    if per_group % 2 == 0 and per_group * row_count == across:
        parts = 4 if per_group % 8 == 0 else 1
        incoming = []
        for part in range(parts):
            given = inverse_cols_half(stacked, row_count, 1 - wl_index, part, parts)
            incoming.append(lax.ppermute(given, "wl", perm=[(0, 1), (1, 0)]))
        incoming = jnp.concatenate(incoming, 2)
        kept = inverse_cols_half(stacked, row_count, wl_index)
    else:
        back = back.reshape((2, row_count, 2, own_rows, width))
        kept = lax.dynamic_index_in_dim(back, wl_index, 2, keepdims=False)
        given = lax.dynamic_index_in_dim(back, 1 - wl_index, 2, keepdims=False)
        incoming = lax.ppermute(given, "wl", perm=[(0, 1), (1, 0)])
    summed = kept + incoming
    returned = lax.all_to_all(summed, "row", split_axis=1, concat_axis=1, tiled=True)
    returned = groups_to_canon(returned, mcount, 1)
    k_half = across // 2
    theirs = inverse_rows(returned, length, norm_factor, k_half, (1 - wl_index) * k_half)
    taken = lax.ppermute(theirs, "wl", perm=[(0, 1), (1, 0)])
    mine = inverse_rows(returned, length, norm_factor, k_half, wl_index * k_half)
    upper = jnp.where(wl_index == 0, mine, taken)
    lower = jnp.where(wl_index == 0, taken, mine)
    return jnp.concatenate([upper, lower], 1)


def solution(mesh):
    in_specs = (P(None, "row", None), P("wl", None, "row", None), P())
    out_specs = P(None, "row", "wl")
    return jax.shard_map(local, mesh=mesh, in_specs=in_specs, out_specs=out_specs, check_vma=False)
```
